512 devices in a mesh: tile: 32 (over y, x, core), depth: 16 (over z).
Axes of the slice: x: 4, y: 4, z: 16, core: 2. Of those that a mesh axis runs over, the one named last changes fastest.
Arguments:
- grid: float32 [4, 128, 128, 1024], P(None, 'tile', 'depth'), may hold values from -6 to 6
- first_moment: float32 [4, 128, 128, 1024], P(None, 'tile', 'depth'), may hold values from -4 to 4
- second_moment: float32 [4, 128, 128, 1024], P(None, 'tile', 'depth'), may hold values from 0.01 to 1
- ray_offset: int32 [128, 1024], P('tile'), may hold values from 0 to 1
- occupancy: int32 [32, 16, 128], P('tile', 'depth'), may hold values 0 or 1
- target: float32 [3, 128, 1024], P(None, 'tile'), may hold values from 0 to 1
Outputs:
- new_grid: float32 [4, 128, 128, 1024], P(None, 'tile', 'depth')
- new_first: float32 [4, 128, 128, 1024], P(None, 'tile', 'depth')
- new_second: float32 [4, 128, 128, 1024], P(None, 'tile', 'depth')
The draws below stay inside these ranges and needn't reach their ends.
All inputs are finite; a program needn't handle non-finite values. No bound on the sum of `occupancy` on one device may be relied on, other than what follows from the above.
Results may differ from the reference program's by a relative error of at most 0.00002.
Values sent between devices are 32-bit elements; how exact they have to be, the bound alone decides.
No kernel may reach another device: no remote copies, remote signals or barrier semaphores. Data moves between devices by JAX's collectives and lax.ppermute only.
A program may use at most 64 MiB of HBM per device.

```python
import math
import jax
import jax.numpy as jnp
from jax import lax

CHANNELS = 4
NX = 128
NY = 1024
NZ = 128


def plant(entries, key, smallest, largest):
    longest = entries.shape.index(max(entries.shape))
    spots = []
    for shift in (0, 1):
        where = [jax.random.randint(jax.random.fold_in(key, axis), (), 0, length) for axis, length in enumerate(entries.shape)]
        where[longest] = (where[longest] + shift) % entries.shape[longest]
        spots.append(tuple(where))
    return entries.at[spots[0]].set(smallest).at[spots[1]].set(largest)


def levels(own_key, dims, cuts, least, top_value):
    factor_of, own = 1.0, jax.random.fold_in(own_key, 6)
    for dim, shards_of in cuts:
        steps = jnp.exp(jax.random.uniform(jax.random.fold_in(own, dim), (shards_of,), jnp.float32, least / len(cuts), top_value / len(cuts)))
        factor_of = factor_of * jnp.repeat(steps, dims[dim] // shards_of).reshape([-1 if axis == dim else 1 for axis in range(len(dims))])
    return factor_of


def gaussian(key, extent, deviation, limit, split=(), kind=jnp.bfloat16):
    drawn = deviation * jax.random.normal(key, extent, jnp.float32)
    if split:
        drawn = drawn * levels(key, extent, split, -0.22, 0.18)
    return jnp.clip(drawn, -limit, limit).astype(kind)


def setup_inputs(seed: int = 0) -> dict:
    seeds = jax.random.split(jax.random.key(seed), 7)
    return {
        "grid": gaussian(seeds[0], (CHANNELS, NX, NZ, NY), 1.0, 6.0, ((1, 32), (2, 16)), jnp.float32),
        "first_moment": gaussian(seeds[1], (CHANNELS, NX, NZ, NY), 0.3, 4.0, ((1, 32), (2, 16)), jnp.float32),
        "second_moment": jnp.clip(jnp.exp(math.log(1.0) - 4.6051702 * jax.random.uniform(seeds[2], (CHANNELS, NX, NZ, NY), jnp.float32) ** levels(seeds[2], (CHANNELS, NX, NZ, NY), ((1, 32), (2, 16)), -0.2, 0.2)), 0.01, 1.0),
        "ray_offset": plant(jax.random.randint(seeds[3], (NX, NY), 0, 2), jax.random.fold_in(seeds[3], 1), 0, 1).astype(jnp.int32),
        "occupancy": plant((jax.random.randint(seeds[4], (NX // 4, NZ // 8, NY // 8), 0, 4) < 3).astype(jnp.int32), jax.random.fold_in(seeds[4], 1), 0, 1),
        "target": jnp.clip(1.0 * jax.random.uniform(seeds[5], (3, NX, NY), jnp.float32) ** levels(seeds[5], (3, NX, NY), ((1, 32),), -0.2, 0.2), 0.0, 1.0),
    }


tv_weight = 0.01
beta_one = 0.9
beta_two = 0.95
learn_rate = 0.1
adam_step = 10
epsilon = 1e-08

def total_loss(grid, ray_offset, occ, target):
    planes = grid.shape[2]
    after_rows = jnp.concatenate([grid[:, 1:], jnp.zeros_like(grid[:, :1])], axis=1)
    shares = (ray_offset.astype(jnp.float32) * 0.5)[None, :, None, :]
    features = (1.0 - shares) * grid + shares * after_rows
    sigma = occ * jax.nn.softplus(features[0]) * (4.0 / planes)
    colour = jax.nn.sigmoid(features[1:])
    before = jnp.cumsum(sigma, axis=1) - sigma
    weight = jnp.exp(-before) * -jnp.expm1(-sigma)
    pixel = lax.optimization_barrier(jnp.sum(weight[None] * colour, axis=2)) + jnp.exp(-lax.optimization_barrier(jnp.sum(sigma, axis=1)))[None]
    loss = 0.25 * planes * jnp.sum((pixel - target) ** 2)
    padded = jnp.pad(grid, ((0, 0), (1, 1), (1, 1), (1, 1)))
    smooth = jnp.sum(jnp.diff(padded, axis=1) ** 2) + jnp.sum(jnp.diff(padded, axis=2) ** 2) + jnp.sum(jnp.diff(padded, axis=3) ** 2)
    return loss + tv_weight * smooth

def reference(grid, first_moment, second_moment, ray_offset, occupancy, target):
    occ = occupancy.astype(jnp.float32)
    occ = jnp.repeat(jnp.repeat(jnp.repeat(occ, 4, axis=0), 8, axis=1), 8, axis=2)
    grad = jax.grad(total_loss)(grid, ray_offset, occ, target)
    new_first = beta_one * first_moment + (1.0 - beta_one) * grad
    new_second = beta_two * second_moment + (1.0 - beta_two) * grad * grad
    corr_one = 1.0 - beta_one ** adam_step
    corr_two = 1.0 - beta_two ** adam_step
    new_grid = grid - learn_rate * (new_first / corr_one) / (jnp.sqrt(new_second / corr_two) + epsilon)
    return (new_grid, new_first, new_second)
```

```python
import jax
import jax.numpy as jnp
from jax import lax
from jax.sharding import PartitionSpec as P

tv_weight = 0.01
beta_one = 0.9
beta_two = 0.95
learn_rate = 0.1
adam_step = 10
epsilon = 1e-08


def carried_in_2(value, axis, join, neutral, backward):
    count, mine = (lax.axis_size(axis), lax.axis_index(axis))
    pieces = jax.tree.map(lambda part: lax.all_gather(part, axis), value)
    if backward:
        pieces = jax.tree.map(lambda part: part[::-1], pieces)
        mine = count - 1 - mine
    total = jax.tree.map(
        lambda part, zero: jnp.full_like(part, 0) + jnp.asarray(zero, part.dtype), value, neutral
    )

    def lap(position, total):
        longer = join(total, jax.tree.map(lambda part: part[position], pieces))
        return jax.tree.map(lambda new, old: jnp.where(position < mine, new, old), longer, total)

    return lax.fori_loop(0, count - 1, lap, total)


def with_halo(cells, sides, width):
    for axis, dim in sides:
        count = lax.axis_size(axis)
        ends = count - 1
        head = lax.slice_in_dim(cells, 0, width, axis=dim)
        tail = lax.slice_in_dim(cells, cells.shape[dim] - width, cells.shape[dim], axis=dim)
        cells = jnp.concatenate(
            [
                lax.ppermute(tail, axis, [(i, (i + 1) % count) for i in range(ends)]),
                cells,
                lax.ppermute(head, axis, [((i + 1) % count, i) for i in range(ends)]),
            ],
            axis=dim,
        )
    return cells


def passed_along(block, axis, distance):
    devices = range(lax.axis_size(axis))
    route = [(i - distance, i) for i in devices if i - distance in devices]
    return lax.ppermute(block, axis, route)


def front_combine(earlier, later):
    return (earlier[0] + earlier[1][None] * later[0], earlier[1] * later[1])


def back_combine(earlier, later):
    return (later[0] + later[1][None] * earlier[0], later[1] * earlier[1])


def over(front, back):
    return jnp.concatenate([front[:-1] + front[-1:] * back[:-1], front[-1:] * back[-1:]], axis=0)


def butterfly_scan(seg_colour, seg_trans, axis):
    count, mine = (lax.axis_size(axis), lax.axis_index(axis))
    block = jnp.concatenate([seg_colour, seg_trans[None]], axis=0)
    blank = jnp.concatenate([jnp.zeros_like(seg_colour), jnp.ones_like(seg_trans)[None]], axis=0)
    prefix, suffix = (blank, blank)
    step = 1
    while step < count:
        other = lax.ppermute(block, axis, [(i, i ^ step) for i in range(count)])
        upper = (mine & step) != 0
        joined = over(jnp.where(upper, other, block), jnp.where(upper, block, other))
        prefix = jnp.where(upper, over(other, prefix), prefix)
        suffix = jnp.where(upper, suffix, over(suffix, other))
        block = joined
        step *= 2
    return (prefix[:-1], prefix[-1], suffix[:-1], suffix[-1])


def render(rows, after_rows, shares, occ, target, total_depth):
    scale = 4.0 / total_depth
    features = (1.0 - shares) * rows + shares * after_rows
    sigma = occ * jax.nn.softplus(features[0]) * scale
    colour = jax.nn.sigmoid(features[1:])
    before = jnp.cumsum(sigma, axis=1) - sigma
    trans = jnp.exp(-before)
    fade = jnp.exp(-sigma)
    weight = trans * -jnp.expm1(-sigma)
    weighted = weight[None] * colour
    seg_colour = jnp.sum(weighted, axis=2)
    seg_trans = jnp.exp(-jnp.sum(sigma, axis=1))
    count = lax.axis_size("depth")
    if count & (count - 1) == 0:
        front_colour, front_trans, back_colour, back_trans = butterfly_scan(
            seg_colour, seg_trans, "depth"
        )
    else:
        blank = (jnp.zeros_like(seg_colour), jnp.ones_like(seg_trans))
        front_colour, front_trans = carried_in_2(
            (seg_colour, seg_trans), "depth", front_combine, blank, False
        )
        back_colour, back_trans = carried_in_2(
            (seg_colour, seg_trans), "depth", back_combine, blank, True
        )
    behind = back_colour + back_trans[None]
    pixel = front_colour + front_trans[None] * (seg_colour + seg_trans[None] * behind)
    pixel_grad = 0.5 * total_depth * (pixel - target)
    upto = jnp.cumsum(weighted, axis=2)
    remain = seg_colour[:, :, None, :] - upto + (seg_trans[None] * behind)[:, :, None, :]
    next_trans = trans * fade
    front_wide = front_trans[:, None, :]
    sigma_grad = front_wide * jnp.sum(
        pixel_grad[:, :, None, :] * (next_trans[None] * colour - remain), axis=0
    )
    colour_grad = front_wide[None] * weight[None] * pixel_grad[:, :, None, :]
    density_grad = sigma_grad * occ * scale * jax.nn.sigmoid(features[0])
    return jnp.concatenate([density_grad[None], colour_grad * colour * (1.0 - colour)], axis=0)


def expand_blocks(blocks):
    return jnp.repeat(jnp.repeat(jnp.repeat(blocks, 4, axis=0), 8, axis=1), 8, axis=2)


def body(grid, first_moment, second_moment, ray_offset, occupancy, target):
    depth_count = lax.axis_size("depth")
    planes = grid.shape[2]
    total_depth = planes * depth_count
    padded = with_halo(grid, (("tile", 1), ("depth", 2)), 1)
    shares = (ray_offset.astype(jnp.float32) * 0.5)[None, :, None, :]
    occ = expand_blocks(occupancy.astype(jnp.float32))
    feature_grad = render(grid, padded[:, 2:, 1:-1, :], shares, occ, target, total_depth)
    carried = shares * feature_grad
    incoming = passed_along(carried[:, -1:], "tile", 1)
    carried_in = jnp.concatenate([incoming, carried[:, :-1]], axis=1)
    data_grad = (1.0 - shares) * feature_grad + carried_in
    across_rows = padded[:, 2:, 1:-1, :] + padded[:, :-2, 1:-1, :]
    across_planes = padded[:, 1:-1, 2:, :] + padded[:, 1:-1, :-2, :]
    side_pad = jnp.pad(grid, ((0, 0), (0, 0), (0, 0), (1, 1)))
    across_cols = side_pad[:, :, :, 2:] + side_pad[:, :, :, :-2]
    smooth_grad = 2.0 * tv_weight * (6.0 * grid - across_rows - across_planes - across_cols)
    grad = data_grad + smooth_grad
    new_first = beta_one * first_moment + (1.0 - beta_one) * grad
    new_second = beta_two * second_moment + (1.0 - beta_two) * grad * grad
    corr_one = 1.0 - beta_one**adam_step
    corr_two = 1.0 - beta_two**adam_step
    new_grid = grid - learn_rate * (new_first / corr_one) / (
        jnp.sqrt(new_second / corr_two) + epsilon
    )
    return (new_grid, new_first, new_second)


def solution(mesh):
    in_specs = (
        P(None, "tile", "depth", None),
        P(None, "tile", "depth", None),
        P(None, "tile", "depth", None),
        P("tile", None),
        P("tile", "depth", None),
        P(None, "tile", None),
    )
    out_specs = (
        P(None, "tile", "depth", None),
        P(None, "tile", "depth", None),
        P(None, "tile", "depth", None),
    )
    return jax.shard_map(body, mesh=mesh, in_specs=in_specs, out_specs=out_specs, check_vma=False)
```

```python
import jax
import jax.numpy as jnp
from jax import lax
from jax.sharding import PartitionSpec as P

tv_weight = 0.01
beta_one = 0.9
beta_two = 0.95
learn_rate = 0.1
adam_step = 10
epsilon = 1e-08


def carried_in_2(value, axis, join, neutral, backward):
    count, mine = (lax.axis_size(axis), lax.axis_index(axis))
    pieces = jax.tree.map(lambda part: lax.all_gather(part, axis), value)
    if backward:
        pieces = jax.tree.map(lambda part: part[::-1], pieces)
        mine = count - 1 - mine
    total = jax.tree.map(
        lambda part, zero: jnp.full_like(part, 0) + jnp.asarray(zero, part.dtype), value, neutral
    )

    def lap(position, total):
        longer = join(total, jax.tree.map(lambda part: part[position], pieces))
        return jax.tree.map(lambda new, old: jnp.where(position < mine, new, old), longer, total)

    return lax.fori_loop(0, count - 1, lap, total)


def with_halo(cells, sides, width):
    for axis, dim in sides:
        count = lax.axis_size(axis)
        ends = count - 1
        head = lax.slice_in_dim(cells, 0, width, axis=dim)
        tail = lax.slice_in_dim(cells, cells.shape[dim] - width, cells.shape[dim], axis=dim)
        cells = jnp.concatenate(
            [
                lax.ppermute(tail, axis, [(i, (i + 1) % count) for i in range(ends)]),
                cells,
                lax.ppermute(head, axis, [((i + 1) % count, i) for i in range(ends)]),
            ],
            axis=dim,
        )
    return cells


def passed_along(block, axis, distance):
    devices = range(lax.axis_size(axis))
    route = [(i - distance, i) for i in devices if i - distance in devices]
    return lax.ppermute(block, axis, route)


def front_combine(earlier, later):
    return (earlier[0] + earlier[1][None] * later[0], earlier[1] * later[1])


def back_combine(earlier, later):
    return (later[0] + later[1][None] * earlier[0], later[1] * earlier[1])


def over(front, back):
    return jnp.concatenate([front[:-1] + front[-1:] * back[:-1], front[-1:] * back[-1:]], axis=0)


def butterfly_scan(seg_colour, seg_trans, axis):
    count, mine = (lax.axis_size(axis), lax.axis_index(axis))
    block = jnp.concatenate([seg_colour, seg_trans[None]], axis=0)
    blank = jnp.concatenate([jnp.zeros_like(seg_colour), jnp.ones_like(seg_trans)[None]], axis=0)
    prefix, suffix = (blank, blank)
    step = 1
    while step < count:
        other = lax.ppermute(block, axis, [(i, i ^ step) for i in range(count)])
        upper = (mine & step) != 0
        joined = over(jnp.where(upper, other, block), jnp.where(upper, block, other))
        prefix = jnp.where(upper, over(other, prefix), prefix)
        suffix = jnp.where(upper, suffix, over(suffix, other))
        block = joined
        step *= 2
    return (prefix[:-1], prefix[-1], suffix[:-1], suffix[-1])


def exchanged_scan(seg_colour, seg_trans, axis):
    count = lax.axis_size(axis)
    shape = seg_trans.shape
    block = jnp.concatenate([seg_colour, seg_trans[None]], axis=0).reshape(4, count, -1)
    mine = lax.all_to_all(block, axis, 1, 1, tiled=True)
    inclusive = lax.associative_scan(over, mine, axis=1)
    flipped = jnp.flip(mine, axis=1)
    behind_incl = jnp.flip(lax.associative_scan(lambda a, b: over(b, a), flipped, axis=1), axis=1)
    blank = jnp.concatenate(
        [jnp.zeros_like(mine[:-1, :1]), jnp.ones_like(mine[-1:, :1])], axis=0
    )
    prefix = jnp.concatenate([blank, inclusive[:, :-1]], axis=1)
    suffix = jnp.concatenate([behind_incl[:, 1:], blank], axis=1)
    total = inclusive[:, -1:]
    pixel = jnp.broadcast_to(total[:-1] + total[-1:], suffix[:-1].shape)
    behind = suffix[:-1] + suffix[-1:]
    answer = jnp.concatenate([prefix[-1:], pixel, behind], axis=0)
    answer = lax.all_to_all(answer, axis, 1, 1, tiled=True).reshape(7, *shape)
    return (answer[0], answer[1:4], answer[4:7])


def render(rows, after_rows, shares, occ, target, total_depth):
    scale = 4.0 / total_depth
    features = (1.0 - shares) * rows + shares * after_rows
    sigma = occ * jax.nn.softplus(features[0]) * scale
    colour = jax.nn.sigmoid(features[1:])
    before = jnp.cumsum(sigma, axis=1) - sigma
    trans = jnp.exp(-before)
    fade = jnp.exp(-sigma)
    weight = trans * -jnp.expm1(-sigma)
    weighted = weight[None] * colour
    seg_colour = jnp.sum(weighted, axis=2)
    seg_trans = jnp.exp(-jnp.sum(sigma, axis=1))
    count = lax.axis_size("depth")
    pixels = seg_trans.size
    if pixels % count == 0 and (pixels // count) % 128 == 0:
        front_trans, pixel, behind = exchanged_scan(seg_colour, seg_trans, "depth")
    elif count & (count - 1) == 0:
        front_colour, front_trans, back_colour, back_trans = butterfly_scan(
            seg_colour, seg_trans, "depth"
        )
    else:
        blank = (jnp.zeros_like(seg_colour), jnp.ones_like(seg_trans))
        front_colour, front_trans = carried_in_2(
            (seg_colour, seg_trans), "depth", front_combine, blank, False
        )
        back_colour, back_trans = carried_in_2(
            (seg_colour, seg_trans), "depth", back_combine, blank, True
        )
    if not (pixels % count == 0 and (pixels // count) % 128 == 0):
        behind = back_colour + back_trans[None]
        pixel = front_colour + front_trans[None] * (seg_colour + seg_trans[None] * behind)
    pixel_grad = 0.5 * total_depth * (pixel - target)
    upto = jnp.cumsum(weighted, axis=2)
    remain = seg_colour[:, :, None, :] - upto + (seg_trans[None] * behind)[:, :, None, :]
    next_trans = trans * fade
    front_wide = front_trans[:, None, :]
    sigma_grad = front_wide * jnp.sum(
        pixel_grad[:, :, None, :] * (next_trans[None] * colour - remain), axis=0
    )
    colour_grad = front_wide[None] * weight[None] * pixel_grad[:, :, None, :]
    density_grad = sigma_grad * occ * scale * jax.nn.sigmoid(features[0])
    return jnp.concatenate([density_grad[None], colour_grad * colour * (1.0 - colour)], axis=0)


def expand_blocks(blocks):
    return jnp.repeat(jnp.repeat(jnp.repeat(blocks, 4, axis=0), 8, axis=1), 8, axis=2)


def body(grid, first_moment, second_moment, ray_offset, occupancy, target):
    depth_count = lax.axis_size("depth")
    planes = grid.shape[2]
    total_depth = planes * depth_count
    padded = with_halo(grid, (("tile", 1), ("depth", 2)), 1)
    shares = (ray_offset.astype(jnp.float32) * 0.5)[None, :, None, :]
    occ = expand_blocks(occupancy.astype(jnp.float32))
    feature_grad = render(grid, padded[:, 2:, 1:-1, :], shares, occ, target, total_depth)
    carried = shares * feature_grad
    incoming = passed_along(carried[:, -1:], "tile", 1)
    carried_in = jnp.concatenate([incoming, carried[:, :-1]], axis=1)
    data_grad = (1.0 - shares) * feature_grad + carried_in
    across_rows = padded[:, 2:, 1:-1, :] + padded[:, :-2, 1:-1, :]
    across_planes = padded[:, 1:-1, 2:, :] + padded[:, 1:-1, :-2, :]
    side_pad = jnp.pad(grid, ((0, 0), (0, 0), (0, 0), (1, 1)))
    across_cols = side_pad[:, :, :, 2:] + side_pad[:, :, :, :-2]
    smooth_grad = 2.0 * tv_weight * (6.0 * grid - across_rows - across_planes - across_cols)
    grad = data_grad + smooth_grad
    new_first = beta_one * first_moment + (1.0 - beta_one) * grad
    new_second = beta_two * second_moment + (1.0 - beta_two) * grad * grad
    corr_one = 1.0 - beta_one**adam_step
    corr_two = 1.0 - beta_two**adam_step
    new_grid = grid - learn_rate * (new_first / corr_one) / (
        jnp.sqrt(new_second / corr_two) + epsilon
    )
    return (new_grid, new_first, new_second)


def solution(mesh):
    in_specs = (
        P(None, "tile", "depth", None),
        P(None, "tile", "depth", None),
        P(None, "tile", "depth", None),
        P("tile", None),
        P("tile", "depth", None),
        P(None, "tile", None),
    )
    out_specs = (
        P(None, "tile", "depth", None),
        P(None, "tile", "depth", None),
        P(None, "tile", "depth", None),
    )
    return jax.shard_map(body, mesh=mesh, in_specs=in_specs, out_specs=out_specs, check_vma=False)
```

```python
import jax
import jax.numpy as jnp
from jax import lax
from jax.sharding import PartitionSpec as P

tv_weight = 0.01
beta_one = 0.9
beta_two = 0.95
learn_rate = 0.1
adam_step = 10
epsilon = 1e-08


def with_halo(cells, sides, width):
    for axis, dim in sides:
        count = lax.axis_size(axis)
        ends = count - 1
        head = lax.slice_in_dim(cells, 0, width, axis=dim)
        tail = lax.slice_in_dim(cells, cells.shape[dim] - width, cells.shape[dim], axis=dim)
        cells = jnp.concatenate(
            [
                lax.ppermute(tail, axis, [(i, (i + 1) % count) for i in range(ends)]),
                cells,
                lax.ppermute(head, axis, [((i + 1) % count, i) for i in range(ends)]),
            ],
            axis=dim,
        )
    return cells


def passed_along(block, axis, distance):
    devices = range(lax.axis_size(axis))
    route = [(i - distance, i) for i in devices if i - distance in devices]
    return lax.ppermute(block, axis, route)


def over(front, back):
    return jnp.concatenate([front[:-1] + front[-1:] * back[:-1], front[-1:] * back[-1:]], axis=0)


def spread(pieces, axis):
    count, mine = (lax.axis_size(axis), lax.axis_index(axis))
    ready = jnp.roll(pieces, -mine, axis=1)
    got = [ready[:, 0]]
    for shift in range(1, count):
        route = [(i, (i + shift) % count) for i in range(count)]
        got.append(lax.ppermute(ready[:, shift], axis, route))
    return jnp.roll(jnp.flip(jnp.stack(got, axis=1), axis=1), mine + 1, axis=1)


def depth_scan(seg_colour, seg_trans, target, total_depth, axis):
    count, mine = (lax.axis_size(axis), lax.axis_index(axis))
    shape = seg_trans.shape
    block = jnp.concatenate([seg_colour, seg_trans[None]], axis=0).reshape(4, count, -1)
    mine_cols = spread(block, axis)
    inclusive = lax.associative_scan(over, mine_cols, axis=1)
    flipped = jnp.flip(mine_cols, axis=1)
    behind_incl = jnp.flip(lax.associative_scan(lambda a, b: over(b, a), flipped, axis=1), axis=1)
    blank = jnp.concatenate(
        [jnp.zeros_like(mine_cols[:-1, :1]), jnp.ones_like(mine_cols[-1:, :1])], axis=0
    )
    prefix = jnp.concatenate([blank, inclusive[:, :-1]], axis=1)
    suffix = jnp.concatenate([behind_incl[:, 1:], blank], axis=1)
    total = inclusive[:, -1]
    pixel = total[:-1] + total[-1:]
    own_target = lax.dynamic_index_in_dim(target.reshape(3, count, -1), mine, axis=1, keepdims=False)
    pixel_grad = 0.5 * total_depth * (pixel - own_target)
    behind = suffix[:-1] + suffix[-1:]
    front_trans = prefix[-1]
    fpg = front_trans[None] * pixel_grad[:, None]
    fback = front_trans * jnp.sum(pixel_grad[:, None] * behind, axis=0)
    answer = spread(jnp.concatenate([fpg, fback[None]], axis=0), axis).reshape(4, *shape)
    return (answer[:3], answer[3])


def render(rows, after_rows, shares, occ, target, total_depth):
    scale = 4.0 / total_depth
    features = (1.0 - shares) * rows + shares * after_rows
    sigma = occ * jax.nn.softplus(features[0]) * scale
    colour = jax.nn.sigmoid(features[1:])
    before = jnp.cumsum(sigma, axis=1) - sigma
    trans = jnp.exp(-before)
    fade = jnp.exp(-sigma)
    weight = trans * -jnp.expm1(-sigma)
    weighted = weight[None] * colour
    seg_colour = jnp.sum(weighted, axis=2)
    seg_trans = jnp.exp(-jnp.sum(sigma, axis=1))
    fpg, fback = depth_scan(seg_colour, seg_trans, target, total_depth, "depth")
    upto = jnp.cumsum(weighted, axis=2)
    next_trans = trans * fade
    sigma_grad = jnp.sum(
        fpg[:, :, None, :] * (next_trans[None] * colour - seg_colour[:, :, None, :] + upto), axis=0
    ) - (seg_trans * fback)[:, None, :]
    colour_grad = weight[None] * fpg[:, :, None, :]
    density_grad = sigma_grad * occ * scale * jax.nn.sigmoid(features[0])
    return jnp.concatenate([density_grad[None], colour_grad * colour * (1.0 - colour)], axis=0)


def expand_blocks(blocks):
    return jnp.repeat(jnp.repeat(jnp.repeat(blocks, 4, axis=0), 8, axis=1), 8, axis=2)


def body(grid, first_moment, second_moment, ray_offset, occupancy, target):
    depth_count = lax.axis_size("depth")
    planes = grid.shape[2]
    total_depth = planes * depth_count
    padded = with_halo(grid, (("tile", 1), ("depth", 2)), 1)
    shares = (ray_offset.astype(jnp.float32) * 0.5)[None, :, None, :]
    occ = expand_blocks(occupancy.astype(jnp.float32))
    feature_grad = render(grid, padded[:, 2:, 1:-1, :], shares, occ, target, total_depth)
    carried = shares * feature_grad
    incoming = passed_along(carried[:, -1:], "tile", 1)
    carried_in = jnp.concatenate([incoming, carried[:, :-1]], axis=1)
    data_grad = (1.0 - shares) * feature_grad + carried_in
    across_rows = padded[:, 2:, 1:-1, :] + padded[:, :-2, 1:-1, :]
    across_planes = padded[:, 1:-1, 2:, :] + padded[:, 1:-1, :-2, :]
    side_pad = jnp.pad(grid, ((0, 0), (0, 0), (0, 0), (1, 1)))
    across_cols = side_pad[:, :, :, 2:] + side_pad[:, :, :, :-2]
    smooth_grad = 2.0 * tv_weight * (6.0 * grid - across_rows - across_planes - across_cols)
    grad = data_grad + smooth_grad
    new_first = beta_one * first_moment + (1.0 - beta_one) * grad
    new_second = beta_two * second_moment + (1.0 - beta_two) * grad * grad
    corr_one = 1.0 - beta_one**adam_step
    corr_two = 1.0 - beta_two**adam_step
    new_grid = grid - learn_rate * (new_first / corr_one) / (
        jnp.sqrt(new_second / corr_two) + epsilon
    )
    return (new_grid, new_first, new_second)


def solution(mesh):
    in_specs = (
        P(None, "tile", "depth", None),
        P(None, "tile", "depth", None),
        P(None, "tile", "depth", None),
        P("tile", None),
        P("tile", "depth", None),
        P(None, "tile", None),
    )
    out_specs = (
        P(None, "tile", "depth", None),
        P(None, "tile", "depth", None),
        P(None, "tile", "depth", None),
    )
    return jax.shard_map(body, mesh=mesh, in_specs=in_specs, out_specs=out_specs, check_vma=False)
```

```python
import jax
import jax.numpy as jnp
from jax import lax
from jax.sharding import PartitionSpec as P

tv_weight = 0.01
beta_one = 0.9
beta_two = 0.95
learn_rate = 0.1
adam_step = 10
epsilon = 1e-08


def carried_in_2(value, axis, join, neutral, backward):
    count, mine = (lax.axis_size(axis), lax.axis_index(axis))
    pieces = jax.tree.map(lambda part: lax.all_gather(part, axis), value)
    if backward:
        pieces = jax.tree.map(lambda part: part[::-1], pieces)
        mine = count - 1 - mine
    total = jax.tree.map(
        lambda part, zero: jnp.full_like(part, 0) + jnp.asarray(zero, part.dtype), value, neutral
    )

    def lap(position, total):
        longer = join(total, jax.tree.map(lambda part: part[position], pieces))
        return jax.tree.map(lambda new, old: jnp.where(position < mine, new, old), longer, total)

    return lax.fori_loop(0, count - 1, lap, total)


def with_halo(cells, sides, width):
    for axis, dim in sides:
        count = lax.axis_size(axis)
        ends = count - 1
        head = lax.slice_in_dim(cells, 0, width, axis=dim)
        tail = lax.slice_in_dim(cells, cells.shape[dim] - width, cells.shape[dim], axis=dim)
        cells = jnp.concatenate(
            [
                lax.ppermute(tail, axis, [(i, (i + 1) % count) for i in range(ends)]),
                cells,
                lax.ppermute(head, axis, [((i + 1) % count, i) for i in range(ends)]),
            ],
            axis=dim,
        )
    return cells


def passed_along(block, axis, distance):
    devices = range(lax.axis_size(axis))
    route = [(i - distance, i) for i in devices if i - distance in devices]
    return lax.ppermute(block, axis, route)


def front_combine(earlier, later):
    return (earlier[0] + earlier[1][None] * later[0], earlier[1] * later[1])


def back_combine(earlier, later):
    return (later[0] + later[1][None] * earlier[0], later[1] * earlier[1])


def over(front, back):
    return jnp.concatenate([front[:-1] + front[-1:] * back[:-1], front[-1:] * back[-1:]], axis=0)


def butterfly_scan(seg_colour, seg_trans, axis):
    count, mine = (lax.axis_size(axis), lax.axis_index(axis))
    block = jnp.concatenate([seg_colour, seg_trans[None]], axis=0)
    blank = jnp.concatenate([jnp.zeros_like(seg_colour), jnp.ones_like(seg_trans)[None]], axis=0)
    prefix, suffix = (blank, blank)
    step = 1
    while step < count:
        other = lax.ppermute(block, axis, [(i, i ^ step) for i in range(count)])
        upper = (mine & step) != 0
        joined = over(jnp.where(upper, other, block), jnp.where(upper, block, other))
        prefix = jnp.where(upper, over(other, prefix), prefix)
        suffix = jnp.where(upper, suffix, over(suffix, other))
        block = joined
        step *= 2
    return (prefix[:-1], prefix[-1], suffix[:-1], suffix[-1])


def render(rows, after_rows, shares, occ, target, total_depth):
    scale = 4.0 / total_depth
    features = (1.0 - shares) * rows + shares * after_rows
    sigma = occ * jax.nn.softplus(features[0]) * scale
    colour = jax.nn.sigmoid(features[1:])
    before = jnp.cumsum(sigma, axis=1) - sigma
    trans = jnp.exp(-before)
    fade = jnp.exp(-sigma)
    weight = trans * -jnp.expm1(-sigma)
    weighted = weight[None] * colour
    seg_colour = jnp.sum(weighted, axis=2)
    seg_trans = jnp.exp(-jnp.sum(sigma, axis=1))
    count = lax.axis_size("depth")
    if count & (count - 1) == 0:
        front_colour, front_trans, back_colour, back_trans = butterfly_scan(
            seg_colour, seg_trans, "depth"
        )
    else:
        blank = (jnp.zeros_like(seg_colour), jnp.ones_like(seg_trans))
        front_colour, front_trans = carried_in_2(
            (seg_colour, seg_trans), "depth", front_combine, blank, False
        )
        back_colour, back_trans = carried_in_2(
            (seg_colour, seg_trans), "depth", back_combine, blank, True
        )
    behind = back_colour + back_trans[None]
    pixel = front_colour + front_trans[None] * (seg_colour + seg_trans[None] * behind)
    pixel_grad = 0.5 * total_depth * (pixel - target)
    upto = jnp.cumsum(weighted, axis=2)
    remain = seg_colour[:, :, None, :] - upto + (seg_trans[None] * behind)[:, :, None, :]
    next_trans = trans * fade
    front_wide = front_trans[:, None, :]
    sigma_grad = front_wide * jnp.sum(
        pixel_grad[:, :, None, :] * (next_trans[None] * colour - remain), axis=0
    )
    colour_grad = front_wide[None] * weight[None] * pixel_grad[:, :, None, :]
    density_grad = sigma_grad * occ * scale * jax.nn.sigmoid(features[0])
    return jnp.concatenate([density_grad[None], colour_grad * colour * (1.0 - colour)], axis=0)


def expand_blocks(blocks):
    return jnp.repeat(jnp.repeat(jnp.repeat(blocks, 4, axis=0), 8, axis=1), 8, axis=2)


def body(grid, first_moment, second_moment, ray_offset, occupancy, target):
    depth_count = lax.axis_size("depth")
    planes = grid.shape[2]
    total_depth = planes * depth_count
    halos = []
    for axis, dim in (("tile", 1), ("depth", 2)):
        count = lax.axis_size(axis)
        head = lax.slice_in_dim(grid, 0, 1, axis=dim)
        tail = lax.slice_in_dim(grid, grid.shape[dim] - 1, grid.shape[dim], axis=dim)
        halos.append(lax.ppermute(tail, axis, [(i, i + 1) for i in range(count - 1)]))
        halos.append(lax.ppermute(head, axis, [(i + 1, i) for i in range(count - 1)]))
    grid, halos = lax.optimization_barrier((grid, halos))
    row_before, row_after, plane_before, plane_after = halos
    rows_after = jnp.concatenate([grid[:, 1:], row_after], axis=1)
    rows_before = jnp.concatenate([row_before, grid[:, :-1]], axis=1)
    planes_after = jnp.concatenate([grid[:, :, 1:], plane_after], axis=2)
    planes_before = jnp.concatenate([plane_before, grid[:, :, :-1]], axis=2)
    shares = (ray_offset.astype(jnp.float32) * 0.5)[None, :, None, :]
    occ = expand_blocks(occupancy.astype(jnp.float32))
    feature_grad = render(grid, rows_after, shares, occ, target, total_depth)
    carried = shares * feature_grad
    incoming = passed_along(carried[:, -1:], "tile", 1)
    carried_in = jnp.concatenate([incoming, carried[:, :-1]], axis=1)
    data_grad = (1.0 - shares) * feature_grad + carried_in
    across_rows = rows_after + rows_before
    across_planes = planes_after + planes_before
    side_pad = jnp.pad(grid, ((0, 0), (0, 0), (0, 0), (1, 1)))
    across_cols = side_pad[:, :, :, 2:] + side_pad[:, :, :, :-2]
    smooth_grad = 2.0 * tv_weight * (6.0 * grid - across_rows - across_planes - across_cols)
    grad = data_grad + smooth_grad
    new_first = beta_one * first_moment + (1.0 - beta_one) * grad
    new_second = beta_two * second_moment + (1.0 - beta_two) * grad * grad
    corr_one = 1.0 - beta_one**adam_step
    corr_two = 1.0 - beta_two**adam_step
    new_grid = grid - learn_rate * (new_first / corr_one) / (
        jnp.sqrt(new_second / corr_two) + epsilon
    )
    return (new_grid, new_first, new_second)


def solution(mesh):
    in_specs = (
        P(None, "tile", "depth", None),
        P(None, "tile", "depth", None),
        P(None, "tile", "depth", None),
        P("tile", None),
        P("tile", "depth", None),
        P(None, "tile", None),
    )
    out_specs = (
        P(None, "tile", "depth", None),
        P(None, "tile", "depth", None),
        P(None, "tile", "depth", None),
    )
    return jax.shard_map(body, mesh=mesh, in_specs=in_specs, out_specs=out_specs, check_vma=False)
```

```python
import jax
import jax.numpy as jnp
from jax import lax
from jax.sharding import PartitionSpec as P

tv_weight = 0.01
beta_one = 0.9
beta_two = 0.95
learn_rate = 0.1
adam_step = 10
epsilon = 1e-08


def carried_in_2(value, axis, join, neutral, backward):
    count, mine = (lax.axis_size(axis), lax.axis_index(axis))
    pieces = jax.tree.map(lambda part: lax.all_gather(part, axis), value)
    if backward:
        pieces = jax.tree.map(lambda part: part[::-1], pieces)
        mine = count - 1 - mine
    total = jax.tree.map(
        lambda part, zero: jnp.full_like(part, 0) + jnp.asarray(zero, part.dtype), value, neutral
    )

    def lap(position, total):
        longer = join(total, jax.tree.map(lambda part: part[position], pieces))
        return jax.tree.map(lambda new, old: jnp.where(position < mine, new, old), longer, total)

    return lax.fori_loop(0, count - 1, lap, total)


def with_halo(cells, sides, width):
    for axis, dim in sides:
        count = lax.axis_size(axis)
        ends = count - 1
        head = lax.slice_in_dim(cells, 0, width, axis=dim)
        tail = lax.slice_in_dim(cells, cells.shape[dim] - width, cells.shape[dim], axis=dim)
        cells = jnp.concatenate(
            [
                lax.ppermute(tail, axis, [(i, (i + 1) % count) for i in range(ends)]),
                cells,
                lax.ppermute(head, axis, [((i + 1) % count, i) for i in range(ends)]),
            ],
            axis=dim,
        )
    return cells


def passed_along(block, axis, distance):
    devices = range(lax.axis_size(axis))
    route = [(i - distance, i) for i in devices if i - distance in devices]
    return lax.ppermute(block, axis, route)


def front_combine(earlier, later):
    return (earlier[0] + earlier[1][None] * later[0], earlier[1] * later[1])


def back_combine(earlier, later):
    return (later[0] + later[1][None] * earlier[0], later[1] * earlier[1])


def over(front, back):
    return jnp.concatenate([front[:-1] + front[-1:] * back[:-1], front[-1:] * back[-1:]], axis=0)


def butterfly_scan(seg_colour, seg_trans, axis):
    count, mine = (lax.axis_size(axis), lax.axis_index(axis))
    block = jnp.concatenate([seg_colour, seg_trans[None]], axis=0)
    blank = jnp.concatenate([jnp.zeros_like(seg_colour), jnp.ones_like(seg_trans)[None]], axis=0)
    prefix, suffix = (blank, blank)
    step = 1
    while step < count:
        route = [(i, i - i % (2 * step) + 2 * step - 1 - i % (2 * step)) for i in range(count)]
        other = lax.ppermute(block, axis, route)
        upper = mine % (2 * step) >= step
        joined = over(jnp.where(upper, other, block), jnp.where(upper, block, other))
        prefix = jnp.where(upper, over(other, prefix), prefix)
        suffix = jnp.where(upper, suffix, over(suffix, other))
        block = joined
        step *= 2
    return (prefix[:-1], prefix[-1], suffix[:-1], suffix[-1])


def render(rows, after_rows, shares, occ, target, total_depth):
    scale = 4.0 / total_depth
    features = (1.0 - shares) * rows + shares * after_rows
    sigma = occ * jax.nn.softplus(features[0]) * scale
    colour = jax.nn.sigmoid(features[1:])
    before = jnp.cumsum(sigma, axis=1) - sigma
    trans = jnp.exp(-before)
    fade = jnp.exp(-sigma)
    weight = trans * -jnp.expm1(-sigma)
    weighted = weight[None] * colour
    seg_colour = jnp.sum(weighted, axis=2)
    seg_trans = jnp.exp(-jnp.sum(sigma, axis=1))
    count = lax.axis_size("depth")
    if count & (count - 1) == 0:
        front_colour, front_trans, back_colour, back_trans = butterfly_scan(
            seg_colour, seg_trans, "depth"
        )
    else:
        blank = (jnp.zeros_like(seg_colour), jnp.ones_like(seg_trans))
        front_colour, front_trans = carried_in_2(
            (seg_colour, seg_trans), "depth", front_combine, blank, False
        )
        back_colour, back_trans = carried_in_2(
            (seg_colour, seg_trans), "depth", back_combine, blank, True
        )
    behind = back_colour + back_trans[None]
    pixel = front_colour + front_trans[None] * (seg_colour + seg_trans[None] * behind)
    pixel_grad = 0.5 * total_depth * (pixel - target)
    upto = jnp.cumsum(weighted, axis=2)
    remain = seg_colour[:, :, None, :] - upto + (seg_trans[None] * behind)[:, :, None, :]
    next_trans = trans * fade
    front_wide = front_trans[:, None, :]
    sigma_grad = front_wide * jnp.sum(
        pixel_grad[:, :, None, :] * (next_trans[None] * colour - remain), axis=0
    )
    colour_grad = front_wide[None] * weight[None] * pixel_grad[:, :, None, :]
    density_grad = sigma_grad * occ * scale * jax.nn.sigmoid(features[0])
    return jnp.concatenate([density_grad[None], colour_grad * colour * (1.0 - colour)], axis=0)


def expand_blocks(blocks):
    return jnp.repeat(jnp.repeat(jnp.repeat(blocks, 4, axis=0), 8, axis=1), 8, axis=2)


def body(grid, first_moment, second_moment, ray_offset, occupancy, target):
    depth_count = lax.axis_size("depth")
    planes = grid.shape[2]
    total_depth = planes * depth_count
    padded = with_halo(grid, (("tile", 1), ("depth", 2)), 1)
    shares = (ray_offset.astype(jnp.float32) * 0.5)[None, :, None, :]
    occ = expand_blocks(occupancy.astype(jnp.float32))
    feature_grad = render(grid, padded[:, 2:, 1:-1, :], shares, occ, target, total_depth)
    carried = shares * feature_grad
    incoming = passed_along(carried[:, -1:], "tile", 1)
    carried_in = jnp.concatenate([incoming, carried[:, :-1]], axis=1)
    data_grad = (1.0 - shares) * feature_grad + carried_in
    across_rows = padded[:, 2:, 1:-1, :] + padded[:, :-2, 1:-1, :]
    across_planes = padded[:, 1:-1, 2:, :] + padded[:, 1:-1, :-2, :]
    side_pad = jnp.pad(grid, ((0, 0), (0, 0), (0, 0), (1, 1)))
    across_cols = side_pad[:, :, :, 2:] + side_pad[:, :, :, :-2]
    smooth_grad = 2.0 * tv_weight * (6.0 * grid - across_rows - across_planes - across_cols)
    grad = data_grad + smooth_grad
    new_first = beta_one * first_moment + (1.0 - beta_one) * grad
    new_second = beta_two * second_moment + (1.0 - beta_two) * grad * grad
    corr_one = 1.0 - beta_one**adam_step
    corr_two = 1.0 - beta_two**adam_step
    new_grid = grid - learn_rate * (new_first / corr_one) / (
        jnp.sqrt(new_second / corr_two) + epsilon
    )
    return (new_grid, new_first, new_second)


def solution(mesh):
    in_specs = (
        P(None, "tile", "depth", None),
        P(None, "tile", "depth", None),
        P(None, "tile", "depth", None),
        P("tile", None),
        P("tile", "depth", None),
        P(None, "tile", None),
    )
    out_specs = (
        P(None, "tile", "depth", None),
        P(None, "tile", "depth", None),
        P(None, "tile", "depth", None),
    )
    return jax.shard_map(body, mesh=mesh, in_specs=in_specs, out_specs=out_specs, check_vma=False)
```

```python
import jax
import jax.numpy as jnp
from jax import lax
from jax.sharding import PartitionSpec as P

tv_weight = 0.01
beta_one = 0.9
beta_two = 0.95
learn_rate = 0.1
adam_step = 10
epsilon = 1e-08


def with_halo(cells, sides, width):
    for axis, dim in sides:
        count = lax.axis_size(axis)
        ends = count - 1
        head = lax.slice_in_dim(cells, 0, width, axis=dim)
        tail = lax.slice_in_dim(cells, cells.shape[dim] - width, cells.shape[dim], axis=dim)
        cells = jnp.concatenate(
            [
                lax.ppermute(tail, axis, [(i, (i + 1) % count) for i in range(ends)]),
                cells,
                lax.ppermute(head, axis, [((i + 1) % count, i) for i in range(ends)]),
            ],
            axis=dim,
        )
    return cells


def passed_along(block, axis, distance):
    devices = range(lax.axis_size(axis))
    route = [(i - distance, i) for i in devices if i - distance in devices]
    return lax.ppermute(block, axis, route)


def over(front, back):
    return jnp.concatenate([front[:-1] + front[-1:] * back[:-1], front[-1:] * back[-1:]], axis=0)


def depth_swap(grid, axis):
    count, mine = (lax.axis_size(axis), lax.axis_index(axis))
    odd = mine % 2 == 1
    route = [(i, i + 1) for i in range(1, count - 1, 2)] + [(i, i - 1) for i in range(2, count, 2)]
    return lax.ppermute(jnp.where(odd, grid[:, :, -1], grid[:, :, 0]), axis, route)


def butterfly_scan(seg_colour, seg_trans, axis, plane_out):
    count, mine = (lax.axis_size(axis), lax.axis_index(axis))
    block = jnp.concatenate([seg_colour, seg_trans[None]], axis=0)
    plane_in = None
    blank = jnp.concatenate([jnp.zeros_like(seg_colour), jnp.ones_like(seg_trans)[None]], axis=0)
    prefix, suffix = (blank, blank)
    step = 1
    while step < count:
        route = [(i, i - i % (2 * step) + 2 * step - 1 - i % (2 * step)) for i in range(count)]
        if step == 1:
            both = lax.ppermute(jnp.concatenate([block, plane_out], axis=0), axis, route)
            other, plane_in = (both[: block.shape[0]], both[block.shape[0] :])
        else:
            other = lax.ppermute(block, axis, route)
        upper = mine % (2 * step) >= step
        joined = over(jnp.where(upper, other, block), jnp.where(upper, block, other))
        prefix = jnp.where(upper, over(other, prefix), prefix)
        suffix = jnp.where(upper, suffix, over(suffix, other))
        block = joined
        step *= 2
    return (prefix[:-1], prefix[-1], suffix[:-1], suffix[-1], plane_in)


def render(rows, after_rows, shares, occ, target, total_depth, plane_out):
    scale = 4.0 / total_depth
    features = (1.0 - shares) * rows + shares * after_rows
    sigma = occ * jax.nn.softplus(features[0]) * scale
    colour = jax.nn.sigmoid(features[1:])
    before = jnp.cumsum(sigma, axis=1) - sigma
    trans = jnp.exp(-before)
    fade = jnp.exp(-sigma)
    weight = trans * -jnp.expm1(-sigma)
    weighted = weight[None] * colour
    seg_colour = jnp.sum(weighted, axis=2)
    seg_trans = jnp.exp(-jnp.sum(sigma, axis=1))
    front_colour, front_trans, back_colour, back_trans, plane_in = butterfly_scan(
        seg_colour, seg_trans, "depth", plane_out
    )
    behind = back_colour + back_trans[None]
    pixel = front_colour + front_trans[None] * (seg_colour + seg_trans[None] * behind)
    pixel_grad = 0.5 * total_depth * (pixel - target)
    upto = jnp.cumsum(weighted, axis=2)
    remain = seg_colour[:, :, None, :] - upto + (seg_trans[None] * behind)[:, :, None, :]
    next_trans = trans * fade
    front_wide = front_trans[:, None, :]
    sigma_grad = front_wide * jnp.sum(
        pixel_grad[:, :, None, :] * (next_trans[None] * colour - remain), axis=0
    )
    colour_grad = front_wide[None] * weight[None] * pixel_grad[:, :, None, :]
    density_grad = sigma_grad * occ * scale * jax.nn.sigmoid(features[0])
    return (jnp.concatenate([density_grad[None], colour_grad * colour * (1.0 - colour)], axis=0), plane_in)


def expand_blocks(blocks):
    return jnp.repeat(jnp.repeat(jnp.repeat(blocks, 4, axis=0), 8, axis=1), 8, axis=2)


def body(grid, first_moment, second_moment, ray_offset, occupancy, target):
    depth_count = lax.axis_size("depth")
    planes = grid.shape[2]
    total_depth = planes * depth_count
    padded = with_halo(grid, (("tile", 1),), 1)
    odd = lax.axis_index("depth") % 2 == 1
    swapped = depth_swap(grid, "depth")
    shares = (ray_offset.astype(jnp.float32) * 0.5)[None, :, None, :]
    occ = expand_blocks(occupancy.astype(jnp.float32))
    plane_out = jnp.where(odd, grid[:, :, 0], grid[:, :, -1])
    feature_grad, plane_in = render(grid, padded[:, 2:], shares, occ, target, total_depth, plane_out)
    plane_before = jnp.where(odd, plane_in, swapped)[:, :, None]
    plane_after = jnp.where(odd, swapped, plane_in)[:, :, None]
    carried = shares * feature_grad
    incoming = passed_along(carried[:, -1:], "tile", 1)
    carried_in = jnp.concatenate([incoming, carried[:, :-1]], axis=1)
    data_grad = (1.0 - shares) * feature_grad + carried_in
    across_rows = padded[:, 2:] + padded[:, :-2]
    across_planes = jnp.concatenate([grid[:, :, 1:], plane_after], axis=2) + jnp.concatenate(
        [plane_before, grid[:, :, :-1]], axis=2
    )
    side_pad = jnp.pad(grid, ((0, 0), (0, 0), (0, 0), (1, 1)))
    across_cols = side_pad[:, :, :, 2:] + side_pad[:, :, :, :-2]
    smooth_grad = 2.0 * tv_weight * (6.0 * grid - across_rows - across_planes - across_cols)
    grad = data_grad + smooth_grad
    new_first = beta_one * first_moment + (1.0 - beta_one) * grad
    new_second = beta_two * second_moment + (1.0 - beta_two) * grad * grad
    corr_one = 1.0 - beta_one**adam_step
    corr_two = 1.0 - beta_two**adam_step
    new_grid = grid - learn_rate * (new_first / corr_one) / (
        jnp.sqrt(new_second / corr_two) + epsilon
    )
    return (new_grid, new_first, new_second)


def solution(mesh):
    in_specs = (
        P(None, "tile", "depth", None),
        P(None, "tile", "depth", None),
        P(None, "tile", "depth", None),
        P("tile", None),
        P("tile", "depth", None),
        P(None, "tile", None),
    )
    out_specs = (
        P(None, "tile", "depth", None),
        P(None, "tile", "depth", None),
        P(None, "tile", "depth", None),
    )
    return jax.shard_map(body, mesh=mesh, in_specs=in_specs, out_specs=out_specs, check_vma=False)
```

```python
import jax
import jax.numpy as jnp
from jax import lax
from jax.sharding import PartitionSpec as P

tv_weight = 0.01
beta_one = 0.9
beta_two = 0.95
learn_rate = 0.1
adam_step = 10
epsilon = 1e-08


def with_halo(cells, sides, width):
    for axis, dim in sides:
        count = lax.axis_size(axis)
        ends = count - 1
        head = lax.slice_in_dim(cells, 0, width, axis=dim)
        tail = lax.slice_in_dim(cells, cells.shape[dim] - width, cells.shape[dim], axis=dim)
        cells = jnp.concatenate(
            [
                lax.ppermute(tail, axis, [(i, (i + 1) % count) for i in range(ends)]),
                cells,
                lax.ppermute(head, axis, [((i + 1) % count, i) for i in range(ends)]),
            ],
            axis=dim,
        )
    return cells


def passed_along(block, axis, distance):
    devices = range(lax.axis_size(axis))
    route = [(i - distance, i) for i in devices if i - distance in devices]
    return lax.ppermute(block, axis, route)


def over(front, back):
    return jnp.concatenate([front[:-1] + front[-1:] * back[:-1], front[-1:] * back[-1:]], axis=0)


def depth_swap(grid, axis):
    count, mine = (lax.axis_size(axis), lax.axis_index(axis))
    odd = mine % 2 == 1
    route = [(i, i + 1) for i in range(1, count - 1, 2)] + [(i, i - 1) for i in range(2, count, 2)]
    return lax.ppermute(jnp.where(odd, grid[:, :, -1], grid[:, :, 0]), axis, route)


def butterfly_scan(seg_colour, seg_trans, axis, plane_out):
    count, mine = (lax.axis_size(axis), lax.axis_index(axis))
    block = jnp.concatenate([seg_colour, seg_trans[None]], axis=0)
    plane_in = None
    blank = jnp.concatenate([jnp.zeros_like(seg_colour), jnp.ones_like(seg_trans)[None]], axis=0)
    prefix, suffix = (blank, blank)
    step = 1
    while step < count:
        route = [(i, i - i % (2 * step) + 2 * step - 1 - i % (2 * step)) for i in range(count)]
        if step == 1:
            both = lax.ppermute(jnp.concatenate([block, plane_out], axis=0), axis, route)
            other, plane_in = (both[: block.shape[0]], both[block.shape[0] :])
        else:
            other = lax.ppermute(block, axis, route)
        upper = mine % (2 * step) >= step
        joined = over(jnp.where(upper, other, block), jnp.where(upper, block, other))
        prefix = jnp.where(upper, over(other, prefix), prefix)
        suffix = jnp.where(upper, suffix, over(suffix, other))
        block = joined
        step *= 2
    return (prefix[:-1], prefix[-1], suffix[:-1], suffix[-1], plane_in)


def render(rows, after_rows, shares, occ, target, total_depth, plane_out):
    scale = 4.0 / total_depth
    features = (1.0 - shares) * rows + shares * after_rows
    sigma = occ * jax.nn.softplus(features[0]) * scale
    colour = jax.nn.sigmoid(features[1:])
    before = jnp.cumsum(sigma, axis=1) - sigma
    trans = jnp.exp(-before)
    fade = jnp.exp(-sigma)
    weight = trans * -jnp.expm1(-sigma)
    weighted = weight[None] * colour
    seg_colour = jnp.sum(weighted, axis=2)
    seg_trans = jnp.exp(-jnp.sum(sigma, axis=1))
    front_colour, front_trans, back_colour, back_trans, plane_in = butterfly_scan(
        seg_colour, seg_trans, "depth", plane_out
    )
    behind = back_colour + back_trans[None]
    pixel = front_colour + front_trans[None] * (seg_colour + seg_trans[None] * behind)

    def backward(rows):
        pixel_grad = 0.5 * total_depth * (pixel[:, rows] - target[:, rows])
        part = weighted[:, rows]
        upto = jnp.cumsum(part, axis=2)
        seg_c = seg_colour[:, rows]
        remain = seg_c[:, :, None, :] - upto + (seg_trans[None, rows] * behind[:, rows])[:, :, None, :]
        next_trans = trans[rows] * fade[rows]
        front_wide = front_trans[rows][:, None, :]
        col = colour[:, rows]
        sigma_grad = front_wide * jnp.sum(
            pixel_grad[:, :, None, :] * (next_trans[None] * col - remain), axis=0
        )
        colour_grad = front_wide[None] * weight[None, rows] * pixel_grad[:, :, None, :]
        density_grad = sigma_grad * occ[rows] * scale * jax.nn.sigmoid(features[0, rows])
        return jnp.concatenate([density_grad[None], colour_grad * col * (1.0 - col)], axis=0)

    last = slice(rows.shape[1] - 1, rows.shape[1])
    return (backward(last), backward(slice(None)), plane_in)


def expand_blocks(blocks):
    return jnp.repeat(jnp.repeat(jnp.repeat(blocks, 4, axis=0), 8, axis=1), 8, axis=2)


def body(grid, first_moment, second_moment, ray_offset, occupancy, target):
    depth_count = lax.axis_size("depth")
    planes = grid.shape[2]
    total_depth = planes * depth_count
    padded = with_halo(grid, (("tile", 1),), 1)
    odd = lax.axis_index("depth") % 2 == 1
    swapped = depth_swap(grid, "depth")
    shares = (ray_offset.astype(jnp.float32) * 0.5)[None, :, None, :]
    occ = expand_blocks(occupancy.astype(jnp.float32))
    plane_out = jnp.where(odd, grid[:, :, 0], grid[:, :, -1])
    last_grad, feature_grad, plane_in = render(
        grid, padded[:, 2:], shares, occ, target, total_depth, plane_out
    )
    plane_before = jnp.where(odd, plane_in, swapped)[:, :, None]
    plane_after = jnp.where(odd, swapped, plane_in)[:, :, None]
    carried = shares * feature_grad
    incoming = passed_along(shares[:, -1:] * last_grad, "tile", 1)
    data_grad = (1.0 - shares) * feature_grad
    across_rows = padded[:, 2:] + padded[:, :-2]
    across_planes = jnp.concatenate([grid[:, :, 1:], plane_after], axis=2) + jnp.concatenate(
        [plane_before, grid[:, :, :-1]], axis=2
    )
    side_pad = jnp.pad(grid, ((0, 0), (0, 0), (0, 0), (1, 1)))
    across_cols = side_pad[:, :, :, 2:] + side_pad[:, :, :, :-2]
    smooth_grad = 2.0 * tv_weight * (6.0 * grid - across_rows - across_planes - across_cols)
    grad = data_grad + jnp.concatenate([jnp.zeros_like(incoming), carried[:, :-1]], axis=1) + smooth_grad
    outs = adam(grid, first_moment, second_moment, grad)
    head_grad = data_grad[:, :1] + incoming + smooth_grad[:, :1]
    heads = adam(grid[:, :1], first_moment[:, :1], second_moment[:, :1], head_grad)
    return tuple(lax.dynamic_update_slice_in_dim(out, head, 0, axis=1) for out, head in zip(outs, heads))


def adam(grid, first_moment, second_moment, grad):
    new_first = beta_one * first_moment + (1.0 - beta_one) * grad
    new_second = beta_two * second_moment + (1.0 - beta_two) * grad * grad
    corr_one = 1.0 - beta_one**adam_step
    corr_two = 1.0 - beta_two**adam_step
    new_grid = grid - learn_rate * (new_first / corr_one) / (
        jnp.sqrt(new_second / corr_two) + epsilon
    )
    return (new_grid, new_first, new_second)


def solution(mesh):
    in_specs = (
        P(None, "tile", "depth", None),
        P(None, "tile", "depth", None),
        P(None, "tile", "depth", None),
        P("tile", None),
        P("tile", "depth", None),
        P(None, "tile", None),
    )
    out_specs = (
        P(None, "tile", "depth", None),
        P(None, "tile", "depth", None),
        P(None, "tile", "depth", None),
    )
    return jax.shard_map(body, mesh=mesh, in_specs=in_specs, out_specs=out_specs, check_vma=False)
```

```python
import jax
import jax.numpy as jnp
from jax import lax
from jax.sharding import PartitionSpec as P

tv_weight = 0.01
beta_one = 0.9
beta_two = 0.95
learn_rate = 0.1
adam_step = 10
epsilon = 1e-08


def over(front, back):
    return jnp.concatenate([front[:-1] + front[-1:] * back[:-1], front[-1:] * back[-1:]], axis=0)


def depth_swap(grid, axis):
    count, mine = (lax.axis_size(axis), lax.axis_index(axis))
    odd = mine % 2 == 1
    route = [(i, i + 1) for i in range(1, count - 1, 2)] + [(i, i - 1) for i in range(2, count, 2)]
    return lax.ppermute(jnp.where(odd, grid[:, :, -1], grid[:, :, 0]), axis, route)


def butterfly_scan(seg_colour, seg_trans, axis, plane_out):
    count, mine = (lax.axis_size(axis), lax.axis_index(axis))
    block = jnp.concatenate([seg_colour, seg_trans[None]], axis=0)
    plane_in = None
    blank = jnp.concatenate([jnp.zeros_like(seg_colour), jnp.ones_like(seg_trans)[None]], axis=0)
    prefix, suffix = (blank, blank)
    step = 1
    while step < count:
        route = [(i, i - i % (2 * step) + 2 * step - 1 - i % (2 * step)) for i in range(count)]
        if step == 1:
            flat = jnp.concatenate([block.reshape(4, -1), plane_out.reshape(4, -1)], axis=1)
            both = lax.ppermute(flat, axis, route)
            other = both[:, : block[0].size].reshape(block.shape)
            plane_in = both[:, block[0].size :].reshape(plane_out.shape)
        else:
            other = lax.ppermute(block, axis, route)
        upper = mine % (2 * step) >= step
        joined = over(jnp.where(upper, other, block), jnp.where(upper, block, other))
        prefix = jnp.where(upper, over(other, prefix), prefix)
        suffix = jnp.where(upper, suffix, over(suffix, other))
        block = joined
        step *= 2
    return (prefix[:-1], prefix[-1], suffix[:-1], suffix[-1], plane_in)


def render(rows, after_rows, shares, occ, target, total_depth, plane_out):
    scale = 4.0 / total_depth
    features = (1.0 - shares) * rows + shares * after_rows
    sigma = occ * jax.nn.softplus(features[0]) * scale
    colour = jax.nn.sigmoid(features[1:])
    before = jnp.cumsum(sigma, axis=1) - sigma
    trans = jnp.exp(-before)
    fade = jnp.exp(-sigma)
    weight = trans * -jnp.expm1(-sigma)
    weighted = weight[None] * colour
    seg_colour = jnp.sum(weighted, axis=2)
    seg_trans = jnp.exp(-jnp.sum(sigma, axis=1))
    front_colour, front_trans, back_colour, back_trans, plane_in = butterfly_scan(
        seg_colour, seg_trans, "depth", plane_out
    )
    behind = back_colour + back_trans[None]
    pixel = front_colour + front_trans[None] * (seg_colour + seg_trans[None] * behind)
    pixel_grad = 0.5 * total_depth * (pixel - target)
    upto = jnp.cumsum(weighted, axis=2)
    remain = seg_colour[:, :, None, :] - upto + (seg_trans[None] * behind)[:, :, None, :]
    next_trans = trans * fade
    front_wide = front_trans[:, None, :]
    sigma_grad = front_wide * jnp.sum(
        pixel_grad[:, :, None, :] * (next_trans[None] * colour - remain), axis=0
    )
    colour_grad = front_wide[None] * weight[None] * pixel_grad[:, :, None, :]
    density_grad = sigma_grad * occ * scale * jax.nn.sigmoid(features[0])
    return (jnp.concatenate([density_grad[None], colour_grad * colour * (1.0 - colour)], axis=0), plane_in)


def expand_blocks(blocks):
    return jnp.repeat(jnp.repeat(jnp.repeat(blocks, 4, axis=0), 8, axis=1), 8, axis=2)


def body(grid, first_moment, second_moment, ray_offset, occupancy, target):
    depth_count = lax.axis_size("depth")
    tiles = lax.axis_size("tile")
    planes = grid.shape[2]
    total_depth = planes * depth_count
    packed = jnp.concatenate(
        [
            grid[:, -1].reshape(-1),
            ray_offset[-1].astype(jnp.float32),
            target[:, -1].reshape(-1),
            occupancy.astype(jnp.float32).reshape(-1),
        ]
    )
    prev = lax.ppermute(packed, "tile", [(i, i + 1) for i in range(tiles - 1)])
    row_after = lax.ppermute(grid[:, :1], "tile", [(i + 1, i) for i in range(tiles - 1)])
    sizes = [grid[:, -1].size, ray_offset.shape[1], target[:, -1].size]
    row_before = prev[: sizes[0]].reshape(grid.shape[0], 1, *grid.shape[2:])
    offset_before = prev[sizes[0] : sizes[0] + sizes[1]].reshape(1, -1)
    target_before = prev[sizes[0] + sizes[1] : sum(sizes)].reshape(target.shape[0], 1, -1)
    occupancy_before = prev[sum(sizes) :].reshape(occupancy.shape)
    odd = lax.axis_index("depth") % 2 == 1
    swapped = depth_swap(grid, "depth")
    ext_rows = jnp.concatenate([row_before, grid], axis=1)
    after_rows = jnp.concatenate([grid, row_after], axis=1)
    shares = (jnp.concatenate([offset_before, ray_offset.astype(jnp.float32)]) * 0.5)[None, :, None, :]
    occ = expand_blocks(occupancy.astype(jnp.float32))
    occ_before = expand_blocks(occupancy_before)[-1:]
    occ_ext = jnp.concatenate([occ_before, occ], axis=0)
    target_ext = jnp.concatenate([target_before, target], axis=1)
    plane_out = jnp.where(odd, grid[:, :, 0], grid[:, :, -1])
    feature_grad, plane_in = render(
        ext_rows, after_rows, shares, occ_ext, target_ext, total_depth, plane_out
    )
    plane_before = jnp.where(odd, plane_in, swapped)[:, :, None]
    plane_after = jnp.where(odd, swapped, plane_in)[:, :, None]
    data_grad = (1.0 - shares[:, 1:]) * feature_grad[:, 1:] + shares[:, :-1] * feature_grad[:, :-1]
    across_rows = after_rows[:, 1:] + ext_rows[:, :-1]
    across_planes = jnp.concatenate([grid[:, :, 1:], plane_after], axis=2) + jnp.concatenate(
        [plane_before, grid[:, :, :-1]], axis=2
    )
    side_pad = jnp.pad(grid, ((0, 0), (0, 0), (0, 0), (1, 1)))
    across_cols = side_pad[:, :, :, 2:] + side_pad[:, :, :, :-2]
    smooth_grad = 2.0 * tv_weight * (6.0 * grid - across_rows - across_planes - across_cols)
    grad = data_grad + smooth_grad
    new_first = beta_one * first_moment + (1.0 - beta_one) * grad
    new_second = beta_two * second_moment + (1.0 - beta_two) * grad * grad
    corr_one = 1.0 - beta_one**adam_step
    corr_two = 1.0 - beta_two**adam_step
    new_grid = grid - learn_rate * (new_first / corr_one) / (
        jnp.sqrt(new_second / corr_two) + epsilon
    )
    return (new_grid, new_first, new_second)


def solution(mesh):
    in_specs = (
        P(None, "tile", "depth", None),
        P(None, "tile", "depth", None),
        P(None, "tile", "depth", None),
        P("tile", None),
        P("tile", "depth", None),
        P(None, "tile", None),
    )
    out_specs = (
        P(None, "tile", "depth", None),
        P(None, "tile", "depth", None),
        P(None, "tile", "depth", None),
    )
    return jax.shard_map(body, mesh=mesh, in_specs=in_specs, out_specs=out_specs, check_vma=False)
```

```python
import jax
import jax.numpy as jnp
from jax import lax
from jax.sharding import PartitionSpec as P

tv_weight = 0.01
beta_one = 0.9
beta_two = 0.95
learn_rate = 0.1
adam_step = 10
epsilon = 1e-08


def passed_along(block, axis, distance):
    devices = range(lax.axis_size(axis))
    route = [(i - distance, i) for i in devices if i - distance in devices]
    return lax.ppermute(block, axis, route)


def over(front, back):
    return jnp.concatenate([front[:-1] + front[-1:] * back[:-1], front[-1:] * back[-1:]], axis=0)


def depth_swap(grid, axis):
    count, mine = (lax.axis_size(axis), lax.axis_index(axis))
    odd = mine % 2 == 1
    route = [(i, i + 1) for i in range(1, count - 1, 2)] + [(i, i - 1) for i in range(2, count, 2)]
    return lax.ppermute(jnp.where(odd, grid[:, :, -1], grid[:, :, 0]), axis, route)


def butterfly_scan(seg_colour, seg_trans, axis, plane_out):
    count, mine = (lax.axis_size(axis), lax.axis_index(axis))
    block = jnp.concatenate([seg_colour, seg_trans[None]], axis=0)
    plane_in = None
    blank = jnp.concatenate([jnp.zeros_like(seg_colour), jnp.ones_like(seg_trans)[None]], axis=0)
    prefix, suffix = (blank, blank)
    step = 1
    while step < count:
        route = [(i, i - i % (2 * step) + 2 * step - 1 - i % (2 * step)) for i in range(count)]
        if step == 1:
            both = lax.ppermute(jnp.concatenate([block, plane_out], axis=0), axis, route)
            other, plane_in = (both[: block.shape[0]], both[block.shape[0] :])
        else:
            other = lax.ppermute(block, axis, route)
        upper = mine % (2 * step) >= step
        joined = over(jnp.where(upper, other, block), jnp.where(upper, block, other))
        prefix = jnp.where(upper, over(other, prefix), prefix)
        suffix = jnp.where(upper, suffix, over(suffix, other))
        block = joined
        step *= 2
    return (prefix[:-1], prefix[-1], suffix[:-1], suffix[-1], plane_in)


def render(rows, after_rows, shares, occ, target, total_depth, plane_out):
    scale = 4.0 / total_depth
    features = (1.0 - shares) * rows + shares * after_rows
    sigma = occ * jax.nn.softplus(features[0]) * scale
    colour = jax.nn.sigmoid(features[1:])
    before = jnp.cumsum(sigma, axis=1) - sigma
    trans = jnp.exp(-before)
    fade = jnp.exp(-sigma)
    weight = trans * -jnp.expm1(-sigma)
    weighted = weight[None] * colour
    seg_colour = jnp.sum(weighted, axis=2)
    seg_trans = jnp.exp(-jnp.sum(sigma, axis=1))
    front_colour, front_trans, back_colour, back_trans, plane_in = butterfly_scan(
        seg_colour, seg_trans, "depth", plane_out
    )
    behind = back_colour + back_trans[None]
    pixel = front_colour + front_trans[None] * (seg_colour + seg_trans[None] * behind)
    pixel_grad = 0.5 * total_depth * (pixel - target)
    upto = jnp.cumsum(weighted, axis=2)
    remain = seg_colour[:, :, None, :] - upto + (seg_trans[None] * behind)[:, :, None, :]
    next_trans = trans * fade
    front_wide = front_trans[:, None, :]
    sigma_grad = front_wide * jnp.sum(
        pixel_grad[:, :, None, :] * (next_trans[None] * colour - remain), axis=0
    )
    colour_grad = front_wide[None] * weight[None] * pixel_grad[:, :, None, :]
    density_grad = sigma_grad * occ * scale * jax.nn.sigmoid(features[0])
    return (jnp.concatenate([density_grad[None], colour_grad * colour * (1.0 - colour)], axis=0), plane_in)


def expand_blocks(blocks):
    return jnp.repeat(jnp.repeat(jnp.repeat(blocks, 4, axis=0), 8, axis=1), 8, axis=2)


def body(grid, first_moment, second_moment, ray_offset, occupancy, target):
    depth_count = lax.axis_size("depth")
    planes = grid.shape[2]
    total_depth = planes * depth_count
    tiles = lax.axis_size("tile")
    row_after = lax.ppermute(grid[:, :1], "tile", [(i + 1, i) for i in range(tiles - 1)])
    rows_after = jnp.concatenate([grid[:, 1:], row_after], axis=1)
    odd = lax.axis_index("depth") % 2 == 1
    swapped = depth_swap(grid, "depth")
    shares = (ray_offset.astype(jnp.float32) * 0.5)[None, :, None, :]
    occ = expand_blocks(occupancy.astype(jnp.float32))
    plane_out = jnp.where(odd, grid[:, :, 0], grid[:, :, -1])
    feature_grad, plane_in = render(grid, rows_after, shares, occ, target, total_depth, plane_out)
    plane_before = jnp.where(odd, plane_in, swapped)[:, :, None]
    plane_after = jnp.where(odd, swapped, plane_in)[:, :, None]
    carried = shares * feature_grad
    both = passed_along(jnp.concatenate([carried[:, -1:], grid[:, -1:]], axis=0), "tile", 1)
    incoming, row_before = (both[: grid.shape[0]], both[grid.shape[0] :])
    carried_in = jnp.concatenate([incoming, carried[:, :-1]], axis=1)
    data_grad = (1.0 - shares) * feature_grad + carried_in
    across_rows = rows_after + jnp.concatenate([row_before, grid[:, :-1]], axis=1)
    across_planes = jnp.concatenate([grid[:, :, 1:], plane_after], axis=2) + jnp.concatenate(
        [plane_before, grid[:, :, :-1]], axis=2
    )
    side_pad = jnp.pad(grid, ((0, 0), (0, 0), (0, 0), (1, 1)))
    across_cols = side_pad[:, :, :, 2:] + side_pad[:, :, :, :-2]
    smooth_grad = 2.0 * tv_weight * (6.0 * grid - across_rows - across_planes - across_cols)
    grad = data_grad + smooth_grad
    new_first = beta_one * first_moment + (1.0 - beta_one) * grad
    new_second = beta_two * second_moment + (1.0 - beta_two) * grad * grad
    corr_one = 1.0 - beta_one**adam_step
    corr_two = 1.0 - beta_two**adam_step
    new_grid = grid - learn_rate * (new_first / corr_one) / (
        jnp.sqrt(new_second / corr_two) + epsilon
    )
    return (new_grid, new_first, new_second)


def solution(mesh):
    in_specs = (
        P(None, "tile", "depth", None),
        P(None, "tile", "depth", None),
        P(None, "tile", "depth", None),
        P("tile", None),
        P("tile", "depth", None),
        P(None, "tile", None),
    )
    out_specs = (
        P(None, "tile", "depth", None),
        P(None, "tile", "depth", None),
        P(None, "tile", "depth", None),
    )
    return jax.shard_map(body, mesh=mesh, in_specs=in_specs, out_specs=out_specs, check_vma=False)
```

```python
import jax
import jax.numpy as jnp
from jax import lax
from jax.sharding import PartitionSpec as P

tv_weight = 0.01
beta_one = 0.9
beta_two = 0.95
learn_rate = 0.1
adam_step = 10
epsilon = 1e-08


def with_halo(cells, sides, width):
    for axis, dim in sides:
        count = lax.axis_size(axis)
        ends = count - 1
        head = lax.slice_in_dim(cells, 0, width, axis=dim)
        tail = lax.slice_in_dim(cells, cells.shape[dim] - width, cells.shape[dim], axis=dim)
        cells = jnp.concatenate(
            [
                lax.ppermute(tail, axis, [(i, (i + 1) % count) for i in range(ends)]),
                cells,
                lax.ppermute(head, axis, [((i + 1) % count, i) for i in range(ends)]),
            ],
            axis=dim,
        )
    return cells


def passed_along(block, axis, distance):
    devices = range(lax.axis_size(axis))
    route = [(i - distance, i) for i in devices if i - distance in devices]
    return lax.ppermute(block, axis, route)


def over(front, back):
    return jnp.concatenate([front[:-1] + front[-1:] * back[:-1], front[-1:] * back[-1:]], axis=0)


def depth_swap(grid, axis):
    count, mine = (lax.axis_size(axis), lax.axis_index(axis))
    odd = mine % 2 == 1
    route = [(i, i + 1) for i in range(1, count - 1, 2)] + [(i, i - 1) for i in range(2, count, 2)]
    return lax.ppermute(jnp.where(odd, grid[:, :, -1], grid[:, :, 0]), axis, route)


def butterfly_scan(seg_colour, seg_trans, axis, plane_out):
    count, mine = (lax.axis_size(axis), lax.axis_index(axis))
    block = jnp.concatenate([seg_colour, seg_trans[None]], axis=0)
    blank = jnp.concatenate([jnp.zeros_like(seg_colour), jnp.ones_like(seg_trans)[None]], axis=0)
    prefix, suffix = (blank, blank)
    plane_in = None
    step = 1
    while step < count and (count // step != 4 or step == 1):
        route = [(i, i - i % (2 * step) + 2 * step - 1 - i % (2 * step)) for i in range(count)]
        if step == 1:
            both = lax.ppermute(jnp.concatenate([block, plane_out], axis=0), axis, route)
            other, plane_in = (both[: block.shape[0]], both[block.shape[0] :])
        else:
            other = lax.ppermute(block, axis, route)
        upper = mine % (2 * step) >= step
        joined = over(jnp.where(upper, other, block), jnp.where(upper, block, other))
        prefix = jnp.where(upper, over(other, prefix), prefix)
        suffix = jnp.where(upper, suffix, over(suffix, other))
        block = joined
        step *= 2
    if step < count:
        group, spot = (mine // step, mine % step)
        routes = (
            [(i, (i // step - 1) % 4 * step + i % step) for i in range(count)],
            [(i, (i // step + 2) % 4 * step + step - 1 - i % step) for i in range(count)],
            [(i, (i // step + 1) % 4 * step + i % step) for i in range(count)],
        )
        got = [lax.ppermute(block, axis, route) for route in routes]
        parts = []
        for j in range(4):
            rel = (j - group) % 4
            parts.append(
                jnp.where(rel == 0, block, jnp.where(rel == 1, got[0], jnp.where(rel == 2, got[1], got[2])))
            )
        front, back = (blank, blank)
        for j in range(4):
            front = jnp.where(j < group, over(front, parts[j]), front)
        for j in reversed(range(4)):
            back = jnp.where(j > group, over(parts[j], back), back)
        prefix = over(front, prefix)
        suffix = over(suffix, back)
    return (prefix[:-1], prefix[-1], suffix[:-1], suffix[-1], plane_in)


def render(rows, after_rows, shares, occ, target, total_depth, plane_out):
    scale = 4.0 / total_depth
    features = (1.0 - shares) * rows + shares * after_rows
    sigma = occ * jax.nn.softplus(features[0]) * scale
    colour = jax.nn.sigmoid(features[1:])
    before = jnp.cumsum(sigma, axis=1) - sigma
    trans = jnp.exp(-before)
    fade = jnp.exp(-sigma)
    weight = trans * -jnp.expm1(-sigma)
    weighted = weight[None] * colour
    seg_colour = jnp.sum(weighted, axis=2)
    seg_trans = jnp.exp(-jnp.sum(sigma, axis=1))
    front_colour, front_trans, back_colour, back_trans, plane_in = butterfly_scan(
        seg_colour, seg_trans, "depth", plane_out
    )
    behind = back_colour + back_trans[None]
    pixel = front_colour + front_trans[None] * (seg_colour + seg_trans[None] * behind)
    pixel_grad = 0.5 * total_depth * (pixel - target)
    upto = jnp.cumsum(weighted, axis=2)
    remain = seg_colour[:, :, None, :] - upto + (seg_trans[None] * behind)[:, :, None, :]
    next_trans = trans * fade
    front_wide = front_trans[:, None, :]
    sigma_grad = front_wide * jnp.sum(
        pixel_grad[:, :, None, :] * (next_trans[None] * colour - remain), axis=0
    )
    colour_grad = front_wide[None] * weight[None] * pixel_grad[:, :, None, :]
    density_grad = sigma_grad * occ * scale * jax.nn.sigmoid(features[0])
    return (jnp.concatenate([density_grad[None], colour_grad * colour * (1.0 - colour)], axis=0), plane_in)


def expand_blocks(blocks):
    return jnp.repeat(jnp.repeat(jnp.repeat(blocks, 4, axis=0), 8, axis=1), 8, axis=2)


def body(grid, first_moment, second_moment, ray_offset, occupancy, target):
    depth_count = lax.axis_size("depth")
    planes = grid.shape[2]
    total_depth = planes * depth_count
    padded = with_halo(grid, (("tile", 1),), 1)
    odd = lax.axis_index("depth") % 2 == 1
    swapped = depth_swap(grid, "depth")
    shares = (ray_offset.astype(jnp.float32) * 0.5)[None, :, None, :]
    occ = expand_blocks(occupancy.astype(jnp.float32))
    plane_out = jnp.where(odd, grid[:, :, 0], grid[:, :, -1])
    feature_grad, plane_in = render(grid, padded[:, 2:], shares, occ, target, total_depth, plane_out)
    plane_before = jnp.where(odd, plane_in, swapped)[:, :, None]
    plane_after = jnp.where(odd, swapped, plane_in)[:, :, None]
    carried = shares * feature_grad
    incoming = passed_along(carried[:, -1:], "tile", 1)
    carried_in = jnp.concatenate([incoming, carried[:, :-1]], axis=1)
    data_grad = (1.0 - shares) * feature_grad + carried_in
    across_rows = padded[:, 2:] + padded[:, :-2]
    across_planes = jnp.concatenate([grid[:, :, 1:], plane_after], axis=2) + jnp.concatenate(
        [plane_before, grid[:, :, :-1]], axis=2
    )
    side_pad = jnp.pad(grid, ((0, 0), (0, 0), (0, 0), (1, 1)))
    across_cols = side_pad[:, :, :, 2:] + side_pad[:, :, :, :-2]
    smooth_grad = 2.0 * tv_weight * (6.0 * grid - across_rows - across_planes - across_cols)
    grad = data_grad + smooth_grad
    new_first = beta_one * first_moment + (1.0 - beta_one) * grad
    new_second = beta_two * second_moment + (1.0 - beta_two) * grad * grad
    corr_one = 1.0 - beta_one**adam_step
    corr_two = 1.0 - beta_two**adam_step
    new_grid = grid - learn_rate * (new_first / corr_one) / (
        jnp.sqrt(new_second / corr_two) + epsilon
    )
    return (new_grid, new_first, new_second)


def solution(mesh):
    in_specs = (
        P(None, "tile", "depth", None),
        P(None, "tile", "depth", None),
        P(None, "tile", "depth", None),
        P("tile", None),
        P("tile", "depth", None),
        P(None, "tile", None),
    )
    out_specs = (
        P(None, "tile", "depth", None),
        P(None, "tile", "depth", None),
        P(None, "tile", "depth", None),
    )
    return jax.shard_map(body, mesh=mesh, in_specs=in_specs, out_specs=out_specs, check_vma=False)
```

```python
import jax
import jax.numpy as jnp
from jax import lax
from jax.sharding import PartitionSpec as P

tv_weight = 0.01
beta_one = 0.9
beta_two = 0.95
learn_rate = 0.1
adam_step = 10
epsilon = 1e-08


def with_halo(cells, sides, width):
    for axis, dim in sides:
        count = lax.axis_size(axis)
        ends = count - 1
        head = lax.slice_in_dim(cells, 0, width, axis=dim)
        tail = lax.slice_in_dim(cells, cells.shape[dim] - width, cells.shape[dim], axis=dim)
        cells = jnp.concatenate(
            [
                lax.ppermute(tail, axis, [(i, (i + 1) % count) for i in range(ends)]),
                cells,
                lax.ppermute(head, axis, [((i + 1) % count, i) for i in range(ends)]),
            ],
            axis=dim,
        )
    return cells


def passed_along(block, axis, distance):
    devices = range(lax.axis_size(axis))
    route = [(i - distance, i) for i in devices if i - distance in devices]
    return lax.ppermute(block, axis, route)


def over(front, back):
    return jnp.concatenate([front[:-1] + front[-1:] * back[:-1], front[-1:] * back[-1:]], axis=0)


def depth_swap(grid, axis):
    count, mine = (lax.axis_size(axis), lax.axis_index(axis))
    odd = mine % 2 == 1
    route = [(i, i + 1) for i in range(1, count - 1, 2)] + [(i, i - 1) for i in range(2, count, 2)]
    return lax.ppermute(jnp.where(odd, grid[:, :, -1], grid[:, :, 0]), axis, route)


def butterfly_scan(seg_colour, seg_trans, axis, plane_out):
    count, mine = (lax.axis_size(axis), lax.axis_index(axis))
    block = jnp.concatenate([seg_colour, seg_trans[None]], axis=0)
    plane_in = None
    blank = jnp.concatenate([jnp.zeros_like(seg_colour), jnp.ones_like(seg_trans)[None]], axis=0)
    prefix, suffix = (blank, blank)
    step = 1
    while step < count:
        route = [(i, i - i % (2 * step) + 2 * step - 1 - i % (2 * step)) for i in range(count)]
        if step == 1:
            both = lax.ppermute(jnp.concatenate([block, plane_out], axis=0), axis, route)
            other, plane_in = (both[: block.shape[0]], both[block.shape[0] :])
        else:
            other = lax.ppermute(block, axis, route)
        upper = mine % (2 * step) >= step
        joined = over(jnp.where(upper, other, block), jnp.where(upper, block, other))
        prefix = jnp.where(upper, over(other, prefix), prefix)
        suffix = jnp.where(upper, suffix, over(suffix, other))
        block = joined
        step *= 2
    return (prefix[:-1], prefix[-1], suffix[:-1], suffix[-1], plane_in)


def render(rows, after_rows, shares, occ, target, total_depth, plane_out):
    scale = 4.0 / total_depth
    features = (1.0 - shares) * rows + shares * after_rows
    sigma = occ * jax.nn.softplus(features[0]) * scale
    colour = jax.nn.sigmoid(features[1:])
    before = jnp.cumsum(sigma, axis=1) - sigma
    trans = jnp.exp(-before)
    fade = jnp.exp(-sigma)
    weight = trans * -jnp.expm1(-sigma)
    weighted = weight[None] * colour
    seg_colour = jnp.sum(weighted, axis=2)
    seg_trans = jnp.exp(-jnp.sum(sigma, axis=1))
    front_colour, front_trans, back_colour, back_trans, plane_in = butterfly_scan(
        seg_colour, seg_trans, "depth", plane_out
    )
    behind = back_colour + back_trans[None]
    pixel = front_colour + front_trans[None] * (seg_colour + seg_trans[None] * behind)

    def backward(pixel, target, weighted, seg_colour, seg_trans, behind, trans, fade, front_trans, colour, weight, occ, density):
        pixel_grad = 0.5 * total_depth * (pixel - target)
        upto = jnp.cumsum(weighted, axis=2)
        remain = seg_colour[:, :, None, :] - upto + (seg_trans[None] * behind)[:, :, None, :]
        next_trans = trans * fade
        front_wide = front_trans[:, None, :]
        sigma_grad = front_wide * jnp.sum(
            pixel_grad[:, :, None, :] * (next_trans[None] * colour - remain), axis=0
        )
        colour_grad = front_wide[None] * weight[None] * pixel_grad[:, :, None, :]
        density_grad = sigma_grad * occ * scale * jax.nn.sigmoid(density)
        return jnp.concatenate([density_grad[None], colour_grad * colour * (1.0 - colour)], axis=0)

    last = rows.shape[1] - 1
    ins = (pixel, target, weighted, seg_colour, seg_trans, behind, trans, fade, front_trans, colour, weight, occ, features[0])
    axes = (1, 1, 1, 1, 0, 1, 0, 0, 0, 1, 0, 0, 0)
    tail = lax.optimization_barrier(tuple(lax.slice_in_dim(x, last, last + 1, axis=k) for x, k in zip(ins, axes)))
    last_grad = backward(*tail)
    full_grad = backward(*ins)
    return (last_grad, full_grad, plane_in)


def expand_blocks(blocks):
    return jnp.repeat(jnp.repeat(jnp.repeat(blocks, 4, axis=0), 8, axis=1), 8, axis=2)


def body(grid, first_moment, second_moment, ray_offset, occupancy, target):
    depth_count = lax.axis_size("depth")
    planes = grid.shape[2]
    total_depth = planes * depth_count
    padded = with_halo(grid, (("tile", 1),), 1)
    odd = lax.axis_index("depth") % 2 == 1
    swapped = depth_swap(grid, "depth")
    shares = (ray_offset.astype(jnp.float32) * 0.5)[None, :, None, :]
    occ = expand_blocks(occupancy.astype(jnp.float32))
    plane_out = jnp.where(odd, grid[:, :, 0], grid[:, :, -1])
    last_grad, feature_grad, plane_in = render(
        grid, padded[:, 2:], shares, occ, target, total_depth, plane_out
    )
    plane_before = jnp.where(odd, plane_in, swapped)[:, :, None]
    plane_after = jnp.where(odd, swapped, plane_in)[:, :, None]
    carried = shares * feature_grad
    incoming = passed_along(shares[:, -1:] * last_grad, "tile", 1)
    carried_in = jnp.concatenate([incoming, carried[:, :-1]], axis=1)
    data_grad = (1.0 - shares) * feature_grad + carried_in
    across_rows = padded[:, 2:] + padded[:, :-2]
    across_planes = jnp.concatenate([grid[:, :, 1:], plane_after], axis=2) + jnp.concatenate(
        [plane_before, grid[:, :, :-1]], axis=2
    )
    side_pad = jnp.pad(grid, ((0, 0), (0, 0), (0, 0), (1, 1)))
    across_cols = side_pad[:, :, :, 2:] + side_pad[:, :, :, :-2]
    smooth_grad = 2.0 * tv_weight * (6.0 * grid - across_rows - across_planes - across_cols)
    grad = data_grad + smooth_grad
    new_first = beta_one * first_moment + (1.0 - beta_one) * grad
    new_second = beta_two * second_moment + (1.0 - beta_two) * grad * grad
    corr_one = 1.0 - beta_one**adam_step
    corr_two = 1.0 - beta_two**adam_step
    new_grid = grid - learn_rate * (new_first / corr_one) / (
        jnp.sqrt(new_second / corr_two) + epsilon
    )
    return (new_grid, new_first, new_second)


def solution(mesh):
    in_specs = (
        P(None, "tile", "depth", None),
        P(None, "tile", "depth", None),
        P(None, "tile", "depth", None),
        P("tile", None),
        P("tile", "depth", None),
        P(None, "tile", None),
    )
    out_specs = (
        P(None, "tile", "depth", None),
        P(None, "tile", "depth", None),
        P(None, "tile", "depth", None),
    )
    return jax.shard_map(body, mesh=mesh, in_specs=in_specs, out_specs=out_specs, check_vma=False)
```

```python
import jax
import jax.numpy as jnp
from jax import lax
from jax.sharding import PartitionSpec as P

tv_weight = 0.01
beta_one = 0.9
beta_two = 0.95
learn_rate = 0.1
adam_step = 10
epsilon = 1e-08


def with_halo(cells, sides, width):
    for axis, dim in sides:
        count = lax.axis_size(axis)
        ends = count - 1
        head = lax.slice_in_dim(cells, 0, width, axis=dim)
        tail = lax.slice_in_dim(cells, cells.shape[dim] - width, cells.shape[dim], axis=dim)
        cells = jnp.concatenate(
            [
                lax.ppermute(tail, axis, [(i, (i + 1) % count) for i in range(ends)]),
                cells,
                lax.ppermute(head, axis, [((i + 1) % count, i) for i in range(ends)]),
            ],
            axis=dim,
        )
    return cells


def passed_along(block, axis, distance):
    devices = range(lax.axis_size(axis))
    route = [(i - distance, i) for i in devices if i - distance in devices]
    return lax.ppermute(block, axis, route)


def over(front, back):
    return jnp.concatenate([front[:-1] + front[-1:] * back[:-1], front[-1:] * back[-1:]], axis=0)


def depth_swap(grid, axis):
    count, mine = (lax.axis_size(axis), lax.axis_index(axis))
    odd = mine % 2 == 1
    route = [(i, i + 1) for i in range(1, count - 1, 2)] + [(i, i - 1) for i in range(2, count, 2)]
    return lax.ppermute(jnp.where(odd, grid[:, :, -1], grid[:, :, 0]), axis, route)


def butterfly_scan(seg_colour, seg_trans, axis, plane_out):
    count, mine = (lax.axis_size(axis), lax.axis_index(axis))
    block = jnp.concatenate([seg_colour, seg_trans[None]], axis=0)
    plane_in = None
    blank = jnp.concatenate([jnp.zeros_like(seg_colour), jnp.ones_like(seg_trans)[None]], axis=0)
    prefix, suffix = (blank, blank)
    step = 1
    while step < count:
        if 2 * step == count:
            route = [(i, count - 1 - i) for i in range(count)]
        else:
            route = [(i, i ^ step) for i in range(count)]
        if step == 1:
            both = lax.ppermute(jnp.concatenate([block, plane_out], axis=0), axis, route)
            other, plane_in = (both[: block.shape[0]], both[block.shape[0] :])
        else:
            other = lax.ppermute(block, axis, route)
        upper = mine % (2 * step) >= step
        joined = over(jnp.where(upper, other, block), jnp.where(upper, block, other))
        prefix = jnp.where(upper, over(other, prefix), prefix)
        suffix = jnp.where(upper, suffix, over(suffix, other))
        block = joined
        step *= 2
    return (prefix[:-1], prefix[-1], suffix[:-1], suffix[-1], plane_in)


def render(rows, after_rows, shares, occ, target, total_depth, plane_out):
    scale = 4.0 / total_depth
    features = (1.0 - shares) * rows + shares * after_rows
    sigma = occ * jax.nn.softplus(features[0]) * scale
    colour = jax.nn.sigmoid(features[1:])
    before = jnp.cumsum(sigma, axis=1) - sigma
    trans = jnp.exp(-before)
    fade = jnp.exp(-sigma)
    weight = trans * -jnp.expm1(-sigma)
    weighted = weight[None] * colour
    seg_colour = jnp.sum(weighted, axis=2)
    seg_trans = jnp.exp(-jnp.sum(sigma, axis=1))
    front_colour, front_trans, back_colour, back_trans, plane_in = butterfly_scan(
        seg_colour, seg_trans, "depth", plane_out
    )
    behind = back_colour + back_trans[None]
    pixel = front_colour + front_trans[None] * (seg_colour + seg_trans[None] * behind)
    pixel_grad = 0.5 * total_depth * (pixel - target)
    upto = jnp.cumsum(weighted, axis=2)
    remain = seg_colour[:, :, None, :] - upto + (seg_trans[None] * behind)[:, :, None, :]
    next_trans = trans * fade
    front_wide = front_trans[:, None, :]
    sigma_grad = front_wide * jnp.sum(
        pixel_grad[:, :, None, :] * (next_trans[None] * colour - remain), axis=0
    )
    colour_grad = front_wide[None] * weight[None] * pixel_grad[:, :, None, :]
    density_grad = sigma_grad * occ * scale * jax.nn.sigmoid(features[0])
    return (jnp.concatenate([density_grad[None], colour_grad * colour * (1.0 - colour)], axis=0), plane_in)


def expand_blocks(blocks):
    return jnp.repeat(jnp.repeat(jnp.repeat(blocks, 4, axis=0), 8, axis=1), 8, axis=2)


def body(grid, first_moment, second_moment, ray_offset, occupancy, target):
    depth_count = lax.axis_size("depth")
    planes = grid.shape[2]
    total_depth = planes * depth_count
    padded = with_halo(grid, (("tile", 1),), 1)
    odd = lax.axis_index("depth") % 2 == 1
    swapped = depth_swap(grid, "depth")
    shares = (ray_offset.astype(jnp.float32) * 0.5)[None, :, None, :]
    occ = expand_blocks(occupancy.astype(jnp.float32))
    plane_out = jnp.where(odd, grid[:, :, 0], grid[:, :, -1])
    feature_grad, plane_in = render(grid, padded[:, 2:], shares, occ, target, total_depth, plane_out)
    plane_before = jnp.where(odd, plane_in, swapped)[:, :, None]
    plane_after = jnp.where(odd, swapped, plane_in)[:, :, None]
    carried = shares * feature_grad
    incoming = passed_along(carried[:, -1:], "tile", 1)
    carried_in = jnp.concatenate([incoming, carried[:, :-1]], axis=1)
    data_grad = (1.0 - shares) * feature_grad + carried_in
    across_rows = padded[:, 2:] + padded[:, :-2]
    across_planes = jnp.concatenate([grid[:, :, 1:], plane_after], axis=2) + jnp.concatenate(
        [plane_before, grid[:, :, :-1]], axis=2
    )
    side_pad = jnp.pad(grid, ((0, 0), (0, 0), (0, 0), (1, 1)))
    across_cols = side_pad[:, :, :, 2:] + side_pad[:, :, :, :-2]
    smooth_grad = 2.0 * tv_weight * (6.0 * grid - across_rows - across_planes - across_cols)
    grad = data_grad + smooth_grad
    new_first = beta_one * first_moment + (1.0 - beta_one) * grad
    new_second = beta_two * second_moment + (1.0 - beta_two) * grad * grad
    corr_one = 1.0 - beta_one**adam_step
    corr_two = 1.0 - beta_two**adam_step
    new_grid = grid - learn_rate * (new_first / corr_one) / (
        jnp.sqrt(new_second / corr_two) + epsilon
    )
    return (new_grid, new_first, new_second)


def solution(mesh):
    in_specs = (
        P(None, "tile", "depth", None),
        P(None, "tile", "depth", None),
        P(None, "tile", "depth", None),
        P("tile", None),
        P("tile", "depth", None),
        P(None, "tile", None),
    )
    out_specs = (
        P(None, "tile", "depth", None),
        P(None, "tile", "depth", None),
        P(None, "tile", "depth", None),
    )
    return jax.shard_map(body, mesh=mesh, in_specs=in_specs, out_specs=out_specs, check_vma=False)
```

```python
import jax
import jax.numpy as jnp
from jax import lax
from jax.sharding import PartitionSpec as P

tv_weight = 0.01
beta_one = 0.9
beta_two = 0.95
learn_rate = 0.1
adam_step = 10
epsilon = 1e-08


def with_halo(cells, sides, width):
    for axis, dim in sides:
        count = lax.axis_size(axis)
        ends = count - 1
        head = lax.slice_in_dim(cells, 0, width, axis=dim)
        tail = lax.slice_in_dim(cells, cells.shape[dim] - width, cells.shape[dim], axis=dim)
        cells = jnp.concatenate(
            [
                lax.ppermute(tail, axis, [(i, (i + 1) % count) for i in range(ends)]),
                cells,
                lax.ppermute(head, axis, [((i + 1) % count, i) for i in range(ends)]),
            ],
            axis=dim,
        )
    return cells


def passed_along(block, axis, distance):
    devices = range(lax.axis_size(axis))
    route = [(i - distance, i) for i in devices if i - distance in devices]
    return lax.ppermute(block, axis, route)


def over(front, back):
    return jnp.concatenate([front[:-1] + front[-1:] * back[:-1], front[-1:] * back[-1:]], axis=0)


def depth_swap(grid, axis):
    count, mine = (lax.axis_size(axis), lax.axis_index(axis))
    odd = mine % 2 == 1
    route = [(i, i + 1) for i in range(1, count - 1, 2)] + [(i, i - 1) for i in range(2, count, 2)]
    return lax.ppermute(jnp.where(odd, grid[:, :, -1], grid[:, :, 0]), axis, route)


def butterfly_scan(seg_colour, seg_trans, axis, plane_out):
    count, mine = (lax.axis_size(axis), lax.axis_index(axis))
    block = jnp.concatenate([seg_colour, seg_trans[None]], axis=0)
    plane_in = None
    blank = jnp.concatenate([block[:-1] * 0.0, block[-1:] * 0.0 + 1.0], axis=0)
    prefix, suffix = (blank, blank)
    step = 1
    while step < count:
        route = [(i, i - i % (2 * step) + 2 * step - 1 - i % (2 * step)) for i in range(count)]
        if step == 1:
            both = lax.ppermute(jnp.concatenate([block, plane_out], axis=0), axis, route)
            other, plane_in = (both[: block.shape[0]], both[block.shape[0] :])
        else:
            other = lax.ppermute(block, axis, route)
        upper = mine % (2 * step) >= step
        joined = over(jnp.where(upper, other, block), jnp.where(upper, block, other))
        prefix = jnp.where(upper, over(other, prefix), prefix)
        suffix = jnp.where(upper, suffix, over(suffix, other))
        block = joined
        step *= 2
    return (prefix[:-1], prefix[-1], suffix[:-1], suffix[-1], plane_in)


def render(rows, after_rows, shares, occ, target, total_depth, plane_out):
    scale = 4.0 / total_depth
    features = (1.0 - shares) * rows + shares * after_rows
    sigma = occ * jax.nn.softplus(features[0]) * scale
    colour = jax.nn.sigmoid(features[1:])
    before = jnp.cumsum(sigma, axis=1) - sigma
    trans = jnp.exp(-before)
    fade = jnp.exp(-sigma)
    weight = trans * -jnp.expm1(-sigma)
    weighted = weight[None] * colour
    seg_colour = jnp.sum(weighted, axis=2)
    seg_trans = jnp.exp(-jnp.sum(sigma, axis=1))
    front_colour, front_trans, back_colour, back_trans, plane_in = butterfly_scan(
        seg_colour, seg_trans, "depth", plane_out
    )
    behind = back_colour + back_trans[None]
    pixel = front_colour + front_trans[None] * (seg_colour + seg_trans[None] * behind)
    pixel_grad = 0.5 * total_depth * (pixel - target)
    upto = jnp.cumsum(weighted, axis=2)
    remain = seg_colour[:, :, None, :] - upto + (seg_trans[None] * behind)[:, :, None, :]
    next_trans = trans * fade
    front_wide = front_trans[:, None, :]
    sigma_grad = front_wide * jnp.sum(
        pixel_grad[:, :, None, :] * (next_trans[None] * colour - remain), axis=0
    )
    colour_grad = front_wide[None] * weight[None] * pixel_grad[:, :, None, :]
    density_grad = sigma_grad * occ * scale * jax.nn.sigmoid(features[0])
    return (jnp.concatenate([density_grad[None], colour_grad * colour * (1.0 - colour)], axis=0), plane_in)


def expand_blocks(blocks):
    return jnp.repeat(jnp.repeat(jnp.repeat(blocks, 4, axis=0), 8, axis=1), 8, axis=2)


def body(grid, first_moment, second_moment, ray_offset, occupancy, target):
    depth_count = lax.axis_size("depth")
    planes = grid.shape[2]
    total_depth = planes * depth_count
    padded = with_halo(grid, (("tile", 1),), 1)
    odd = lax.axis_index("depth") % 2 == 1
    swapped = depth_swap(grid, "depth")
    shares = (ray_offset.astype(jnp.float32) * 0.5)[None, :, None, :]
    occ = expand_blocks(occupancy.astype(jnp.float32))
    plane_out = jnp.where(odd, grid[:, :, 0], grid[:, :, -1])
    feature_grad, plane_in = render(grid, padded[:, 2:], shares, occ, target, total_depth, plane_out)
    plane_before = jnp.where(odd, plane_in, swapped)[:, :, None]
    plane_after = jnp.where(odd, swapped, plane_in)[:, :, None]
    carried = shares * feature_grad
    incoming = passed_along(carried[:, -1:], "tile", 1)
    carried_in = jnp.concatenate([incoming, carried[:, :-1]], axis=1)
    data_grad = (1.0 - shares) * feature_grad + carried_in
    across_rows = padded[:, 2:] + padded[:, :-2]
    across_planes = jnp.concatenate([grid[:, :, 1:], plane_after], axis=2) + jnp.concatenate(
        [plane_before, grid[:, :, :-1]], axis=2
    )
    side_pad = jnp.pad(grid, ((0, 0), (0, 0), (0, 0), (1, 1)))
    across_cols = side_pad[:, :, :, 2:] + side_pad[:, :, :, :-2]
    smooth_grad = 2.0 * tv_weight * (6.0 * grid - across_rows - across_planes - across_cols)
    grad = data_grad + smooth_grad
    new_first = beta_one * first_moment + (1.0 - beta_one) * grad
    new_second = beta_two * second_moment + (1.0 - beta_two) * grad * grad
    corr_one = 1.0 - beta_one**adam_step
    corr_two = 1.0 - beta_two**adam_step
    new_grid = grid - learn_rate * (new_first / corr_one) / (
        jnp.sqrt(new_second / corr_two) + epsilon
    )
    return (new_grid, new_first, new_second)


def solution(mesh):
    in_specs = (
        P(None, "tile", "depth", None),
        P(None, "tile", "depth", None),
        P(None, "tile", "depth", None),
        P("tile", None),
        P("tile", "depth", None),
        P(None, "tile", None),
    )
    out_specs = (
        P(None, "tile", "depth", None),
        P(None, "tile", "depth", None),
        P(None, "tile", "depth", None),
    )
    return jax.shard_map(body, mesh=mesh, in_specs=in_specs, out_specs=out_specs, check_vma=False)
```

```python
import jax
import jax.numpy as jnp
from jax import lax
from jax.sharding import PartitionSpec as P

tv_weight = 0.01
beta_one = 0.9
beta_two = 0.95
learn_rate = 0.1
adam_step = 10
epsilon = 1e-08


def passed_along(block, axis, distance):
    devices = range(lax.axis_size(axis))
    route = [(i - distance, i) for i in devices if i - distance in devices]
    return lax.ppermute(block, axis, route)


def over(front, back):
    return jnp.concatenate([front[:-1] + front[-1:] * back[:-1], front[-1:] * back[-1:]], axis=0)


def depth_swap(grid, axis):
    count, mine = (lax.axis_size(axis), lax.axis_index(axis))
    odd = mine % 2 == 1
    route = [(i, i + 1) for i in range(1, count - 1, 2)] + [(i, i - 1) for i in range(2, count, 2)]
    return lax.ppermute(jnp.where(odd, grid[:, :, -1], grid[:, :, 0]), axis, route)


def butterfly_scan(seg_colour, seg_trans, axis, plane_out):
    count, mine = (lax.axis_size(axis), lax.axis_index(axis))
    block = jnp.concatenate([seg_colour, seg_trans[None]], axis=0)
    plane_in = None
    blank = jnp.concatenate([block[:-1] * 0.0, block[-1:] * 0.0 + 1.0], axis=0)
    prefix, suffix = (blank, blank)
    step = 1
    while step < count:
        route = [(i, i - i % (2 * step) + 2 * step - 1 - i % (2 * step)) for i in range(count)]
        if step == 1:
            both = lax.ppermute(jnp.concatenate([block, plane_out], axis=0), axis, route)
            other, plane_in = (both[: block.shape[0]], both[block.shape[0] :])
        else:
            other = lax.ppermute(block, axis, route)
        upper = mine % (2 * step) >= step
        joined = over(jnp.where(upper, other, block), jnp.where(upper, block, other))
        prefix = jnp.where(upper, over(other, prefix), prefix)
        suffix = jnp.where(upper, suffix, over(suffix, other))
        block = joined
        step *= 2
    return (prefix[:-1], prefix[-1], suffix[:-1], suffix[-1], plane_in)


def render(rows, after_rows, shares, occ, target, total_depth, plane_out):
    scale = 4.0 / total_depth
    features = (1.0 - shares) * rows + shares * after_rows
    sigma = occ * jax.nn.softplus(features[0]) * scale
    colour = jax.nn.sigmoid(features[1:])
    before = jnp.cumsum(sigma, axis=1) - sigma
    trans = jnp.exp(-before)
    fade = jnp.exp(-sigma)
    weight = trans * -jnp.expm1(-sigma)
    weighted = weight[None] * colour
    seg_colour = jnp.sum(weighted, axis=2)
    seg_trans = jnp.exp(-jnp.sum(sigma, axis=1))
    front_colour, front_trans, back_colour, back_trans, plane_in = butterfly_scan(
        seg_colour, seg_trans, "depth", plane_out
    )
    behind = back_colour + back_trans[None]
    pixel = front_colour + front_trans[None] * (seg_colour + seg_trans[None] * behind)
    pixel_grad = 0.5 * total_depth * (pixel - target)
    upto = jnp.cumsum(weighted, axis=2)
    remain = seg_colour[:, :, None, :] - upto + (seg_trans[None] * behind)[:, :, None, :]
    next_trans = trans * fade
    front_wide = front_trans[:, None, :]
    sigma_grad = front_wide * jnp.sum(
        pixel_grad[:, :, None, :] * (next_trans[None] * colour - remain), axis=0
    )
    colour_grad = front_wide[None] * weight[None] * pixel_grad[:, :, None, :]
    density_grad = sigma_grad * occ * scale * jax.nn.sigmoid(features[0])
    return (jnp.concatenate([density_grad[None], colour_grad * colour * (1.0 - colour)], axis=0), plane_in)


def expand_blocks(blocks):
    return jnp.repeat(jnp.repeat(jnp.repeat(blocks, 4, axis=0), 8, axis=1), 8, axis=2)


def body(grid, first_moment, second_moment, ray_offset, occupancy, target):
    depth_count = lax.axis_size("depth")
    planes = grid.shape[2]
    total_depth = planes * depth_count
    tiles = lax.axis_size("tile")
    row_after = lax.ppermute(grid[:, :1], "tile", [(i + 1, i) for i in range(tiles - 1)])
    rows_after = jnp.concatenate([grid[:, 1:], row_after], axis=1)
    odd = lax.axis_index("depth") % 2 == 1
    swapped = depth_swap(grid, "depth")
    shares = (ray_offset.astype(jnp.float32) * 0.5)[None, :, None, :]
    occ = expand_blocks(occupancy.astype(jnp.float32))
    plane_out = jnp.where(odd, grid[:, :, 0], grid[:, :, -1])
    feature_grad, plane_in = render(grid, rows_after, shares, occ, target, total_depth, plane_out)
    plane_before = jnp.where(odd, plane_in, swapped)[:, :, None]
    plane_after = jnp.where(odd, swapped, plane_in)[:, :, None]
    carried = shares * feature_grad
    incoming = passed_along(carried[:, -1:] - 2.0 * tv_weight * grid[:, -1:], "tile", 1)
    carried_in = jnp.concatenate([incoming, carried[:, :-1]], axis=1)
    data_grad = (1.0 - shares) * feature_grad + carried_in
    across_rows = rows_after + jnp.concatenate([jnp.zeros_like(grid[:, :1]), grid[:, :-1]], axis=1)
    across_planes = jnp.concatenate([grid[:, :, 1:], plane_after], axis=2) + jnp.concatenate(
        [plane_before, grid[:, :, :-1]], axis=2
    )
    side_pad = jnp.pad(grid, ((0, 0), (0, 0), (0, 0), (1, 1)))
    across_cols = side_pad[:, :, :, 2:] + side_pad[:, :, :, :-2]
    smooth_grad = 2.0 * tv_weight * (6.0 * grid - across_rows - across_planes - across_cols)
    grad = data_grad + smooth_grad
    new_first = beta_one * first_moment + (1.0 - beta_one) * grad
    new_second = beta_two * second_moment + (1.0 - beta_two) * grad * grad
    corr_one = 1.0 - beta_one**adam_step
    corr_two = 1.0 - beta_two**adam_step
    new_grid = grid - learn_rate * (new_first / corr_one) / (
        jnp.sqrt(new_second / corr_two) + epsilon
    )
    return (new_grid, new_first, new_second)


def solution(mesh):
    in_specs = (
        P(None, "tile", "depth", None),
        P(None, "tile", "depth", None),
        P(None, "tile", "depth", None),
        P("tile", None),
        P("tile", "depth", None),
        P(None, "tile", None),
    )
    out_specs = (
        P(None, "tile", "depth", None),
        P(None, "tile", "depth", None),
        P(None, "tile", "depth", None),
    )
    return jax.shard_map(body, mesh=mesh, in_specs=in_specs, out_specs=out_specs, check_vma=False)
```

```python
import jax
import jax.numpy as jnp
from jax import lax
from jax.sharding import PartitionSpec as P

tv_weight = 0.01
beta_one = 0.9
beta_two = 0.95
learn_rate = 0.1
adam_step = 10
epsilon = 1e-08


def with_halo(cells, sides, width):
    for axis, dim in sides:
        count = lax.axis_size(axis)
        ends = count - 1
        head = lax.slice_in_dim(cells, 0, width, axis=dim)
        tail = lax.slice_in_dim(cells, cells.shape[dim] - width, cells.shape[dim], axis=dim)
        cells = jnp.concatenate(
            [
                lax.ppermute(tail, axis, [(i, (i + 1) % count) for i in range(ends)]),
                cells,
                lax.ppermute(head, axis, [((i + 1) % count, i) for i in range(ends)]),
            ],
            axis=dim,
        )
    return cells


def passed_along(block, axis, distance):
    devices = range(lax.axis_size(axis))
    route = [(i - distance, i) for i in devices if i - distance in devices]
    return lax.ppermute(block, axis, route)


def over(front, back):
    return jnp.concatenate([front[:-1] + front[-1:] * back[:-1], front[-1:] * back[-1:]], axis=0)


def depth_swap(grid, axis):
    count, mine = (lax.axis_size(axis), lax.axis_index(axis))
    odd = mine % 2 == 1
    route = [(i, i + 1) for i in range(1, count - 1, 2)] + [(i, i - 1) for i in range(2, count, 2)]
    return lax.ppermute(jnp.where(odd, grid[:, :, -1], grid[:, :, 0]), axis, route)


def butterfly_scan(seg_colour, seg_trans, axis, plane_out):
    count, mine = (lax.axis_size(axis), lax.axis_index(axis))
    block = jnp.concatenate([seg_colour, seg_trans[None]], axis=0)
    plane_in = None
    blank = jnp.concatenate([block[:-1] * 0.0, block[-1:] * 0.0 + 1.0], axis=0)
    prefix, suffix = (blank, blank)
    step = 1
    while step < count:
        if step == 2:
            route = [(i, i ^ step) for i in range(count)]
        else:
            route = [(i, i - i % (2 * step) + 2 * step - 1 - i % (2 * step)) for i in range(count)]
        if step == 1:
            both = lax.ppermute(jnp.concatenate([block, plane_out], axis=0), axis, route)
            other, plane_in = (both[: block.shape[0]], both[block.shape[0] :])
        else:
            other = lax.ppermute(block, axis, route)
        upper = mine % (2 * step) >= step
        joined = over(jnp.where(upper, other, block), jnp.where(upper, block, other))
        prefix = jnp.where(upper, over(other, prefix), prefix)
        suffix = jnp.where(upper, suffix, over(suffix, other))
        block = joined
        step *= 2
    return (prefix[:-1], prefix[-1], suffix[:-1], suffix[-1], plane_in)


def render(rows, after_rows, shares, occ, target, total_depth, plane_out):
    scale = 4.0 / total_depth
    features = (1.0 - shares) * rows + shares * after_rows
    sigma = occ * jax.nn.softplus(features[0]) * scale
    colour = jax.nn.sigmoid(features[1:])
    before = jnp.cumsum(sigma, axis=1) - sigma
    trans = jnp.exp(-before)
    fade = jnp.exp(-sigma)
    weight = trans * -jnp.expm1(-sigma)
    weighted = weight[None] * colour
    seg_colour = jnp.sum(weighted, axis=2)
    seg_trans = jnp.exp(-jnp.sum(sigma, axis=1))
    front_colour, front_trans, back_colour, back_trans, plane_in = butterfly_scan(
        seg_colour, seg_trans, "depth", plane_out
    )
    behind = back_colour + back_trans[None]
    pixel = front_colour + front_trans[None] * (seg_colour + seg_trans[None] * behind)
    pixel_grad = 0.5 * total_depth * (pixel - target)
    upto = jnp.cumsum(weighted, axis=2)
    remain = seg_colour[:, :, None, :] - upto + (seg_trans[None] * behind)[:, :, None, :]
    next_trans = trans * fade
    front_wide = front_trans[:, None, :]
    sigma_grad = front_wide * jnp.sum(
        pixel_grad[:, :, None, :] * (next_trans[None] * colour - remain), axis=0
    )
    colour_grad = front_wide[None] * weight[None] * pixel_grad[:, :, None, :]
    density_grad = sigma_grad * occ * scale * jax.nn.sigmoid(features[0])
    return (jnp.concatenate([density_grad[None], colour_grad * colour * (1.0 - colour)], axis=0), plane_in)


def expand_blocks(blocks):
    return jnp.repeat(jnp.repeat(jnp.repeat(blocks, 4, axis=0), 8, axis=1), 8, axis=2)


def body(grid, first_moment, second_moment, ray_offset, occupancy, target):
    depth_count = lax.axis_size("depth")
    planes = grid.shape[2]
    total_depth = planes * depth_count
    padded = with_halo(grid, (("tile", 1),), 1)
    odd = lax.axis_index("depth") % 2 == 1
    swapped = depth_swap(grid, "depth")
    shares = (ray_offset.astype(jnp.float32) * 0.5)[None, :, None, :]
    occ = expand_blocks(occupancy.astype(jnp.float32))
    plane_out = jnp.where(odd, grid[:, :, 0], grid[:, :, -1])
    feature_grad, plane_in = render(grid, padded[:, 2:], shares, occ, target, total_depth, plane_out)
    plane_before = jnp.where(odd, plane_in, swapped)[:, :, None]
    plane_after = jnp.where(odd, swapped, plane_in)[:, :, None]
    carried = shares * feature_grad
    incoming = passed_along(carried[:, -1:], "tile", 1)
    carried_in = jnp.concatenate([incoming, carried[:, :-1]], axis=1)
    data_grad = (1.0 - shares) * feature_grad + carried_in
    across_rows = padded[:, 2:] + padded[:, :-2]
    across_planes = jnp.concatenate([grid[:, :, 1:], plane_after], axis=2) + jnp.concatenate(
        [plane_before, grid[:, :, :-1]], axis=2
    )
    side_pad = jnp.pad(grid, ((0, 0), (0, 0), (0, 0), (1, 1)))
    across_cols = side_pad[:, :, :, 2:] + side_pad[:, :, :, :-2]
    smooth_grad = 2.0 * tv_weight * (6.0 * grid - across_rows - across_planes - across_cols)
    grad = data_grad + smooth_grad
    new_first = beta_one * first_moment + (1.0 - beta_one) * grad
    new_second = beta_two * second_moment + (1.0 - beta_two) * grad * grad
    corr_one = 1.0 - beta_one**adam_step
    corr_two = 1.0 - beta_two**adam_step
    new_grid = grid - learn_rate * (new_first / corr_one) / (
        jnp.sqrt(new_second / corr_two) + epsilon
    )
    return (new_grid, new_first, new_second)


def solution(mesh):
    in_specs = (
        P(None, "tile", "depth", None),
        P(None, "tile", "depth", None),
        P(None, "tile", "depth", None),
        P("tile", None),
        P("tile", "depth", None),
        P(None, "tile", None),
    )
    out_specs = (
        P(None, "tile", "depth", None),
        P(None, "tile", "depth", None),
        P(None, "tile", "depth", None),
    )
    return jax.shard_map(body, mesh=mesh, in_specs=in_specs, out_specs=out_specs, check_vma=False)
```

```python
import jax
import jax.numpy as jnp
from jax import lax
from jax.sharding import PartitionSpec as P

tv_weight = 0.01
beta_one = 0.9
beta_two = 0.95
learn_rate = 0.1
adam_step = 10
epsilon = 1e-08


def with_halo(cells, sides, width):
    for axis, dim in sides:
        count = lax.axis_size(axis)
        ends = count - 1
        head = lax.slice_in_dim(cells, 0, width, axis=dim)
        tail = lax.slice_in_dim(cells, cells.shape[dim] - width, cells.shape[dim], axis=dim)
        cells = jnp.concatenate(
            [
                lax.ppermute(tail, axis, [(i, (i + 1) % count) for i in range(ends)]),
                cells,
                lax.ppermute(head, axis, [((i + 1) % count, i) for i in range(ends)]),
            ],
            axis=dim,
        )
    return cells


def passed_along(block, axis, distance):
    devices = range(lax.axis_size(axis))
    route = [(i - distance, i) for i in devices if i - distance in devices]
    return lax.ppermute(block, axis, route)


def over(front, back):
    return jnp.concatenate([front[:-1] + front[-1:] * back[:-1], front[-1:] * back[-1:]], axis=0)


def depth_swap(grid, axis):
    count, mine = (lax.axis_size(axis), lax.axis_index(axis))
    odd = mine % 2 == 1
    route = [(i, i + 1) for i in range(1, count - 1, 2)] + [(i, i - 1) for i in range(2, count, 2)]
    return lax.ppermute(jnp.where(odd, grid[:, :, -1], grid[:, :, 0]), axis, route)


def butterfly_scan(seg_colour, seg_trans, axis, plane_out):
    count, mine = (lax.axis_size(axis), lax.axis_index(axis))
    block = jnp.concatenate([seg_colour, seg_trans[None]], axis=0)
    plane_in = None
    blank = jnp.concatenate([block[:-1] * 0.0, block[-1:] * 0.0 + 1.0], axis=0)
    prefix, suffix = (blank, blank)
    step = 1
    while step < count:
        route = [(i, i - i % (2 * step) + 2 * step - 1 - i % (2 * step)) for i in range(count)]
        if step == 1:
            both = lax.ppermute(jnp.concatenate([block, plane_out], axis=0), axis, route)
            other, plane_in = (both[: block.shape[0]], both[block.shape[0] :])
        else:
            other = lax.ppermute(block, axis, route)
        upper = mine % (2 * step) >= step
        joined = over(jnp.where(upper, other, block), jnp.where(upper, block, other))
        prefix = jnp.where(upper, over(other, prefix), prefix)
        suffix = jnp.where(upper, suffix, over(suffix, other))
        block = joined
        step *= 2
    return (prefix[:-1], prefix[-1], suffix[:-1], suffix[-1], plane_in)


def render(rows, after_rows, shares, occ, target, total_depth, plane_out):
    scale = 4.0 / total_depth
    features = (1.0 - shares) * rows + shares * after_rows
    sigma = occ * jax.nn.softplus(features[0]) * scale
    colour = jax.nn.sigmoid(features[1:])
    before = jnp.cumsum(sigma, axis=1) - sigma
    trans = jnp.exp(-before)
    fade = jnp.exp(-sigma)
    weight = trans * -jnp.expm1(-sigma)
    weighted = weight[None] * colour
    seg_colour = jnp.sum(weighted, axis=2)
    seg_trans = jnp.exp(-jnp.sum(sigma, axis=1))
    scaled_target, seg_colour = lax.optimization_barrier((0.5 * total_depth * target, seg_colour))
    front_colour, front_trans, back_colour, back_trans, plane_in = butterfly_scan(
        seg_colour, seg_trans, "depth", plane_out
    )
    behind = back_colour + back_trans[None]
    pixel = front_colour + front_trans[None] * (seg_colour + seg_trans[None] * behind)
    pixel_grad = 0.5 * total_depth * pixel - scaled_target
    upto = jnp.cumsum(weighted, axis=2)
    remain = seg_colour[:, :, None, :] - upto + (seg_trans[None] * behind)[:, :, None, :]
    next_trans = trans * fade
    front_wide = front_trans[:, None, :]
    sigma_grad = front_wide * jnp.sum(
        pixel_grad[:, :, None, :] * (next_trans[None] * colour - remain), axis=0
    )
    colour_grad = front_wide[None] * weight[None] * pixel_grad[:, :, None, :]
    density_grad = sigma_grad * occ * scale * jax.nn.sigmoid(features[0])
    return (jnp.concatenate([density_grad[None], colour_grad * colour * (1.0 - colour)], axis=0), plane_in)


def expand_blocks(blocks):
    return jnp.repeat(jnp.repeat(jnp.repeat(blocks, 4, axis=0), 8, axis=1), 8, axis=2)


def body(grid, first_moment, second_moment, ray_offset, occupancy, target):
    depth_count = lax.axis_size("depth")
    planes = grid.shape[2]
    total_depth = planes * depth_count
    padded = with_halo(grid, (("tile", 1),), 1)
    odd = lax.axis_index("depth") % 2 == 1
    swapped = depth_swap(grid, "depth")
    shares = (ray_offset.astype(jnp.float32) * 0.5)[None, :, None, :]
    occ = expand_blocks(occupancy.astype(jnp.float32))
    plane_out = jnp.where(odd, grid[:, :, 0], grid[:, :, -1])
    feature_grad, plane_in = render(grid, padded[:, 2:], shares, occ, target, total_depth, plane_out)
    plane_before = jnp.where(odd, plane_in, swapped)[:, :, None]
    plane_after = jnp.where(odd, swapped, plane_in)[:, :, None]
    carried = shares * feature_grad
    incoming = passed_along(carried[:, -1:], "tile", 1)
    carried_in = jnp.concatenate([incoming, carried[:, :-1]], axis=1)
    data_grad = (1.0 - shares) * feature_grad + carried_in
    across_rows = padded[:, 2:] + padded[:, :-2]
    across_planes = jnp.concatenate([grid[:, :, 1:], plane_after], axis=2) + jnp.concatenate(
        [plane_before, grid[:, :, :-1]], axis=2
    )
    side_pad = jnp.pad(grid, ((0, 0), (0, 0), (0, 0), (1, 1)))
    across_cols = side_pad[:, :, :, 2:] + side_pad[:, :, :, :-2]
    smooth_grad = 2.0 * tv_weight * (6.0 * grid - across_rows - across_planes - across_cols)
    grad = data_grad + smooth_grad
    new_first = beta_one * first_moment + (1.0 - beta_one) * grad
    new_second = beta_two * second_moment + (1.0 - beta_two) * grad * grad
    corr_one = 1.0 - beta_one**adam_step
    corr_two = 1.0 - beta_two**adam_step
    new_grid = grid - learn_rate * (new_first / corr_one) / (
        jnp.sqrt(new_second / corr_two) + epsilon
    )
    return (new_grid, new_first, new_second)


def solution(mesh):
    in_specs = (
        P(None, "tile", "depth", None),
        P(None, "tile", "depth", None),
        P(None, "tile", "depth", None),
        P("tile", None),
        P("tile", "depth", None),
        P(None, "tile", None),
    )
    out_specs = (
        P(None, "tile", "depth", None),
        P(None, "tile", "depth", None),
        P(None, "tile", "depth", None),
    )
    return jax.shard_map(body, mesh=mesh, in_specs=in_specs, out_specs=out_specs, check_vma=False)
```

```python
import jax
import jax.numpy as jnp
from jax import lax
from jax.sharding import PartitionSpec as P

tv_weight = 0.01
beta_one = 0.9
beta_two = 0.95
learn_rate = 0.1
adam_step = 10
epsilon = 1e-08


def with_halo(cells, sides, width):
    for axis, dim in sides:
        count = lax.axis_size(axis)
        ends = count - 1
        head = lax.slice_in_dim(cells, 0, width, axis=dim)
        tail = lax.slice_in_dim(cells, cells.shape[dim] - width, cells.shape[dim], axis=dim)
        cells = jnp.concatenate(
            [
                lax.ppermute(tail, axis, [(i, (i + 1) % count) for i in range(ends)]),
                cells,
                lax.ppermute(head, axis, [((i + 1) % count, i) for i in range(ends)]),
            ],
            axis=dim,
        )
    return cells


def passed_along(block, axis, distance):
    devices = range(lax.axis_size(axis))
    route = [(i - distance, i) for i in devices if i - distance in devices]
    return lax.ppermute(block, axis, route)


def over(front, back):
    return jnp.concatenate([front[:-1] + front[-1:] * back[:-1], front[-1:] * back[-1:]], axis=0)


def depth_swap(grid, axis):
    count, mine = (lax.axis_size(axis), lax.axis_index(axis))
    odd = mine % 2 == 1
    route = [(i, i + 1) for i in range(1, count - 1, 2)] + [(i, i - 1) for i in range(2, count, 2)]
    return lax.ppermute(jnp.where(odd, grid[:, :, -1], grid[:, :, 0]), axis, route)


def butterfly_scan(seg_colour, seg_trans, axis, plane_out):
    count, mine = (lax.axis_size(axis), lax.axis_index(axis))
    block = jnp.concatenate([seg_colour, seg_trans[None]], axis=0)
    plane_in = None
    blank = jnp.concatenate([block[:-1] * 0.0, block[-1:] * 0.0 + 1.0], axis=0)
    prefix, suffix = (blank, blank)
    step = 1
    while step < count:
        route = [(i, i - i % (2 * step) + 2 * step - 1 - i % (2 * step)) for i in range(count)]
        if step == 1:
            both = lax.ppermute(jnp.concatenate([block, plane_out], axis=0), axis, route)
            other, plane_in = (both[: block.shape[0]], both[block.shape[0] :])
        else:
            other = lax.ppermute(block, axis, route)
        upper = mine % (2 * step) >= step
        joined = over(jnp.where(upper, other, block), jnp.where(upper, block, other))
        prefix = jnp.where(upper, over(other, prefix), prefix)
        suffix = jnp.where(upper, suffix, over(suffix, other))
        block = joined
        step *= 2
    return (prefix[:-1], prefix[-1], suffix[:-1], suffix[-1], plane_in)


def render(rows, after_rows, shares, occ, target, total_depth, plane_out):
    scale = 4.0 / total_depth
    features = (1.0 - shares) * rows + shares * after_rows
    sigma = occ * jax.nn.softplus(features[0]) * scale
    colour = jax.nn.sigmoid(features[1:])
    before = jnp.cumsum(sigma, axis=1) - sigma
    trans = jnp.exp(-before)
    fade = jnp.exp(-sigma)
    weight = trans * -jnp.expm1(-sigma)
    weighted = weight[None] * colour
    seg_colour = jnp.sum(weighted, axis=2)
    seg_trans = jnp.exp(-jnp.sum(sigma, axis=1))
    scaled_target, seg_colour = lax.optimization_barrier((0.5 * total_depth * target, seg_colour))
    front_colour, front_trans, back_colour, back_trans, plane_in = butterfly_scan(
        seg_colour, seg_trans, "depth", plane_out
    )
    behind = back_colour + back_trans[None]
    pixel = front_colour + front_trans[None] * (seg_colour + seg_trans[None] * behind)
    pixel_grad = 0.5 * total_depth * pixel - scaled_target
    upto = jnp.cumsum(weighted, axis=2)
    remain = seg_colour[:, :, None, :] - upto + (seg_trans[None] * behind)[:, :, None, :]
    next_trans = trans * fade
    front_wide = front_trans[:, None, :]
    sigma_grad = front_wide * jnp.sum(
        pixel_grad[:, :, None, :] * (next_trans[None] * colour - remain), axis=0
    )
    colour_grad = front_wide[None] * weight[None] * pixel_grad[:, :, None, :]
    density_grad = sigma_grad * occ * scale * jax.nn.sigmoid(features[0])
    return (jnp.concatenate([density_grad[None], colour_grad * colour * (1.0 - colour)], axis=0), plane_in)


def expand_blocks(blocks):
    return jnp.repeat(jnp.repeat(jnp.repeat(blocks, 4, axis=0), 8, axis=1), 8, axis=2)


def body(grid, first_moment, second_moment, ray_offset, occupancy, target):
    depth_count = lax.axis_size("depth")
    planes = grid.shape[2]
    total_depth = planes * depth_count
    tiles = lax.axis_size("tile")
    row_after = lax.ppermute(grid[:, :1], "tile", [(i + 1, i) for i in range(tiles - 1)])
    last_row, row_after = lax.optimization_barrier((grid[:, -1:], row_after))
    row_before = lax.ppermute(last_row, "tile", [(i, i + 1) for i in range(tiles - 1)])
    padded = jnp.concatenate([row_before, grid, row_after], axis=1)
    odd = lax.axis_index("depth") % 2 == 1
    swapped = depth_swap(grid, "depth")
    shares = (ray_offset.astype(jnp.float32) * 0.5)[None, :, None, :]
    occ = expand_blocks(occupancy.astype(jnp.float32))
    plane_out = jnp.where(odd, grid[:, :, 0], grid[:, :, -1])
    feature_grad, plane_in = render(grid, padded[:, 2:], shares, occ, target, total_depth, plane_out)
    plane_before = jnp.where(odd, plane_in, swapped)[:, :, None]
    plane_after = jnp.where(odd, swapped, plane_in)[:, :, None]
    carried = shares * feature_grad
    incoming = passed_along(carried[:, -1:], "tile", 1)
    carried_in = jnp.concatenate([incoming, carried[:, :-1]], axis=1)
    data_grad = (1.0 - shares) * feature_grad + carried_in
    across_rows = padded[:, 2:] + padded[:, :-2]
    across_planes = jnp.concatenate([grid[:, :, 1:], plane_after], axis=2) + jnp.concatenate(
        [plane_before, grid[:, :, :-1]], axis=2
    )
    side_pad = jnp.pad(grid, ((0, 0), (0, 0), (0, 0), (1, 1)))
    across_cols = side_pad[:, :, :, 2:] + side_pad[:, :, :, :-2]
    smooth_grad = 2.0 * tv_weight * (6.0 * grid - across_rows - across_planes - across_cols)
    grad = data_grad + smooth_grad
    new_first = beta_one * first_moment + (1.0 - beta_one) * grad
    new_second = beta_two * second_moment + (1.0 - beta_two) * grad * grad
    corr_one = 1.0 - beta_one**adam_step
    corr_two = 1.0 - beta_two**adam_step
    new_grid = grid - learn_rate * (new_first / corr_one) / (
        jnp.sqrt(new_second / corr_two) + epsilon
    )
    return (new_grid, new_first, new_second)


def solution(mesh):
    in_specs = (
        P(None, "tile", "depth", None),
        P(None, "tile", "depth", None),
        P(None, "tile", "depth", None),
        P("tile", None),
        P("tile", "depth", None),
        P(None, "tile", None),
    )
    out_specs = (
        P(None, "tile", "depth", None),
        P(None, "tile", "depth", None),
        P(None, "tile", "depth", None),
    )
    return jax.shard_map(body, mesh=mesh, in_specs=in_specs, out_specs=out_specs, check_vma=False)
```

```python
import jax
import jax.numpy as jnp
from jax import lax
from jax.sharding import PartitionSpec as P

tv_weight = 0.01
beta_one = 0.9
beta_two = 0.95
learn_rate = 0.1
adam_step = 10
epsilon = 1e-08


def with_halo(cells, sides, width):
    for axis, dim in sides:
        count = lax.axis_size(axis)
        ends = count - 1
        head = lax.slice_in_dim(cells, 0, width, axis=dim)
        tail = lax.slice_in_dim(cells, cells.shape[dim] - width, cells.shape[dim], axis=dim)
        cells = jnp.concatenate(
            [
                lax.ppermute(tail, axis, [(i, (i + 1) % count) for i in range(ends)]),
                cells,
                lax.ppermute(head, axis, [((i + 1) % count, i) for i in range(ends)]),
            ],
            axis=dim,
        )
    return cells


def passed_along(block, axis, distance):
    devices = range(lax.axis_size(axis))
    route = [(i - distance, i) for i in devices if i - distance in devices]
    return lax.ppermute(block, axis, route)


def over(front, back):
    return jnp.concatenate([front[:-1] + front[-1:] * back[:-1], front[-1:] * back[-1:]], axis=0)


def depth_swap(grid, axis):
    count, mine = (lax.axis_size(axis), lax.axis_index(axis))
    odd = mine % 2 == 1
    route = [(i, i + 1) for i in range(1, count - 1, 2)] + [(i, i - 1) for i in range(2, count, 2)]
    return lax.ppermute(jnp.where(odd, grid[:, :, -1], grid[:, :, 0]), axis, route)


def butterfly_scan(seg_colour, seg_trans, axis, plane_out):
    count, mine = (lax.axis_size(axis), lax.axis_index(axis))
    block = jnp.concatenate([seg_colour, seg_trans[None]], axis=0)
    plane_in = None
    blank = jnp.concatenate([block[:-1] * 0.0, block[-1:] * 0.0 + 1.0], axis=0)
    prefix, suffix = (blank, blank)
    step = 1
    while step < count:
        route = [(i, i - i % (2 * step) + 2 * step - 1 - i % (2 * step)) for i in range(count)]
        if step == 1:
            both = lax.ppermute(jnp.concatenate([block, plane_out], axis=0), axis, route)
            other, plane_in = (both[: block.shape[0]], both[block.shape[0] :])
        else:
            other = lax.ppermute(block, axis, route)
        upper = mine % (2 * step) >= step
        joined = over(jnp.where(upper, other, block), jnp.where(upper, block, other))
        prefix = jnp.where(upper, over(other, prefix), prefix)
        suffix = jnp.where(upper, suffix, over(suffix, other))
        block = joined
        step *= 2
    return (prefix[:-1], prefix[-1], suffix[:-1], suffix[-1], plane_in)


def render(rows, after_rows, shares, occ, target, total_depth, plane_out):
    scale = 4.0 / total_depth
    features = (1.0 - shares) * rows + shares * after_rows
    sigma = occ * jax.nn.softplus(features[0]) * scale
    colour = jax.nn.sigmoid(features[1:])
    before = jnp.cumsum(sigma, axis=1) - sigma
    trans = jnp.exp(-before)
    fade = jnp.exp(-sigma)
    weight = trans * -jnp.expm1(-sigma)
    weighted = weight[None] * colour
    seg_colour = jnp.sum(weighted, axis=2)
    seg_trans = jnp.exp(-jnp.sum(sigma, axis=1))
    scaled_target, seg_colour = lax.optimization_barrier((0.5 * total_depth * target, seg_colour))
    front_colour, front_trans, back_colour, back_trans, plane_in = butterfly_scan(
        seg_colour, seg_trans, "depth", plane_out
    )
    behind = back_colour + back_trans[None]
    pixel = front_colour + front_trans[None] * (seg_colour + seg_trans[None] * behind)
    pixel_grad = 0.5 * total_depth * pixel - scaled_target
    upto = jnp.cumsum(weighted, axis=2)
    remain = seg_colour[:, :, None, :] - upto + (seg_trans[None] * behind)[:, :, None, :]
    next_trans = trans * fade
    front_wide = front_trans[:, None, :]
    sigma_grad = front_wide * jnp.sum(
        pixel_grad[:, :, None, :] * (next_trans[None] * colour - remain), axis=0
    )
    colour_grad = front_wide[None] * weight[None] * pixel_grad[:, :, None, :]
    density_grad = sigma_grad * occ * scale * jax.nn.sigmoid(features[0])
    return (jnp.concatenate([density_grad[None], colour_grad * colour * (1.0 - colour)], axis=0), plane_in)


def expand_blocks(blocks):
    return jnp.repeat(jnp.repeat(jnp.repeat(blocks, 4, axis=0), 8, axis=1), 8, axis=2)


def body(grid, first_moment, second_moment, ray_offset, occupancy, target):
    depth_count = lax.axis_size("depth")
    planes = grid.shape[2]
    total_depth = planes * depth_count
    padded = with_halo(grid, (("tile", 1),), 1)
    odd = lax.axis_index("depth") % 2 == 1
    swapped = depth_swap(grid, "depth")
    shares = (ray_offset.astype(jnp.float32) * 0.5)[None, :, None, :]
    occ = expand_blocks(occupancy.astype(jnp.float32))
    first_moment, second_moment, occ = lax.optimization_barrier((first_moment, second_moment, occ))
    plane_out = jnp.where(odd, grid[:, :, 0], grid[:, :, -1])
    feature_grad, plane_in = render(grid, padded[:, 2:], shares, occ, target, total_depth, plane_out)
    plane_before = jnp.where(odd, plane_in, swapped)[:, :, None]
    plane_after = jnp.where(odd, swapped, plane_in)[:, :, None]
    carried = shares * feature_grad
    incoming = passed_along(carried[:, -1:], "tile", 1)
    carried_in = jnp.concatenate([incoming, carried[:, :-1]], axis=1)
    data_grad = (1.0 - shares) * feature_grad + carried_in
    across_rows = padded[:, 2:] + padded[:, :-2]
    across_planes = jnp.concatenate([grid[:, :, 1:], plane_after], axis=2) + jnp.concatenate(
        [plane_before, grid[:, :, :-1]], axis=2
    )
    side_pad = jnp.pad(grid, ((0, 0), (0, 0), (0, 0), (1, 1)))
    across_cols = side_pad[:, :, :, 2:] + side_pad[:, :, :, :-2]
    smooth_grad = 2.0 * tv_weight * (6.0 * grid - across_rows - across_planes - across_cols)
    grad = data_grad + smooth_grad
    new_first = beta_one * first_moment + (1.0 - beta_one) * grad
    new_second = beta_two * second_moment + (1.0 - beta_two) * grad * grad
    corr_one = 1.0 - beta_one**adam_step
    corr_two = 1.0 - beta_two**adam_step
    new_grid = grid - learn_rate * (new_first / corr_one) / (
        jnp.sqrt(new_second / corr_two) + epsilon
    )
    return (new_grid, new_first, new_second)


def solution(mesh):
    in_specs = (
        P(None, "tile", "depth", None),
        P(None, "tile", "depth", None),
        P(None, "tile", "depth", None),
        P("tile", None),
        P("tile", "depth", None),
        P(None, "tile", None),
    )
    out_specs = (
        P(None, "tile", "depth", None),
        P(None, "tile", "depth", None),
        P(None, "tile", "depth", None),
    )
    return jax.shard_map(body, mesh=mesh, in_specs=in_specs, out_specs=out_specs, check_vma=False)
```

```python
import jax
import jax.numpy as jnp
from jax import lax
from jax.sharding import PartitionSpec as P

tv_weight = 0.01
beta_one = 0.9
beta_two = 0.95
learn_rate = 0.1
adam_step = 10
epsilon = 1e-08


def with_halo(cells, sides, width):
    for axis, dim in sides:
        count = lax.axis_size(axis)
        ends = count - 1
        head = lax.slice_in_dim(cells, 0, width, axis=dim)
        tail = lax.slice_in_dim(cells, cells.shape[dim] - width, cells.shape[dim], axis=dim)
        cells = jnp.concatenate(
            [
                lax.ppermute(tail, axis, [(i, (i + 1) % count) for i in range(ends)]),
                cells,
                lax.ppermute(head, axis, [((i + 1) % count, i) for i in range(ends)]),
            ],
            axis=dim,
        )
    return cells


def passed_along(block, axis, distance):
    devices = range(lax.axis_size(axis))
    route = [(i - distance, i) for i in devices if i - distance in devices]
    return lax.ppermute(block, axis, route)


def over(front, back):
    return jnp.concatenate([front[:-1] + front[-1:] * back[:-1], front[-1:] * back[-1:]], axis=0)


def depth_swap(grid, axis):
    count, mine = (lax.axis_size(axis), lax.axis_index(axis))
    odd = mine % 2 == 1
    route = [(i, i + 1) for i in range(1, count - 1, 2)] + [(i, i - 1) for i in range(2, count, 2)]
    return lax.ppermute(jnp.where(odd, grid[:, :, -1], grid[:, :, 0]), axis, route)


def butterfly_scan(seg_colour, seg_trans, axis, plane_out):
    count, mine = (lax.axis_size(axis), lax.axis_index(axis))
    block = jnp.concatenate([seg_colour, seg_trans[None]], axis=0)
    plane_in = None
    blank = jnp.concatenate([block[:-1] * 0.0, block[-1:] * 0.0 + 1.0], axis=0)
    prefix, suffix = (blank, blank)
    step = 1
    while step < count:
        route = [(i, i - i % (2 * step) + 2 * step - 1 - i % (2 * step)) for i in range(count)]
        if step == 1:
            both = lax.ppermute(jnp.concatenate([block, plane_out], axis=0), axis, route)
            other, plane_in = (both[: block.shape[0]], both[block.shape[0] :])
        else:
            other = lax.ppermute(block, axis, route)
        upper = mine % (2 * step) >= step
        joined = over(jnp.where(upper, other, block), jnp.where(upper, block, other))
        prefix = jnp.where(upper, over(other, prefix), prefix)
        suffix = jnp.where(upper, suffix, over(suffix, other))
        block = joined
        step *= 2
    return (prefix[:-1], prefix[-1], suffix[:-1], suffix[-1], plane_in)


def render(rows, after_rows, shares, occ, target, total_depth, plane_out):
    scale = 4.0 / total_depth
    features = (1.0 - shares) * rows + shares * after_rows
    sigma = occ * jax.nn.softplus(features[0]) * scale
    colour = jax.nn.sigmoid(features[1:])
    before = jnp.cumsum(sigma, axis=1) - sigma
    trans = jnp.exp(-before)
    fade = jnp.exp(-sigma)
    weight = trans * -jnp.expm1(-sigma)
    weighted = weight[None] * colour
    seg_colour = jnp.sum(weighted, axis=2)
    seg_trans = jnp.exp(-jnp.sum(sigma, axis=1))
    scaled_target, seg_colour = lax.optimization_barrier((0.5 * total_depth * target, seg_colour))
    front_colour, front_trans, back_colour, back_trans, plane_in = butterfly_scan(
        seg_colour, seg_trans, "depth", plane_out
    )
    behind = back_colour + back_trans[None]
    pixel = front_colour + front_trans[None] * (seg_colour + seg_trans[None] * behind)
    pixel_grad = 0.5 * total_depth * pixel - scaled_target
    upto = jnp.cumsum(weighted, axis=2)
    remain = seg_colour[:, :, None, :] - upto + (seg_trans[None] * behind)[:, :, None, :]
    next_trans = trans * fade
    front_wide = front_trans[:, None, :]
    sigma_grad = front_wide * jnp.sum(
        pixel_grad[:, :, None, :] * (next_trans[None] * colour - remain), axis=0
    )
    colour_grad = front_wide[None] * weight[None] * pixel_grad[:, :, None, :]
    density_grad = sigma_grad * occ * scale * jax.nn.sigmoid(features[0])
    return (jnp.concatenate([density_grad[None], colour_grad * colour * (1.0 - colour)], axis=0), plane_in)


def expand_blocks(blocks):
    return jnp.repeat(jnp.repeat(jnp.repeat(blocks, 4, axis=0), 8, axis=1), 8, axis=2)


def body(grid, first_moment, second_moment, ray_offset, occupancy, target):
    depth_count = lax.axis_size("depth")
    planes = grid.shape[2]
    total_depth = planes * depth_count
    tiles = lax.axis_size("tile")
    row_after = lax.ppermute(grid[:, :1], "tile", [(i + 1, i) for i in range(tiles - 1)])
    last_row, row_after = lax.optimization_barrier((grid[:, -1:], row_after))
    row_before = lax.ppermute(last_row, "tile", [(i, i + 1) for i in range(tiles - 1)])
    padded = jnp.concatenate([row_before, grid, row_after], axis=1)
    odd = lax.axis_index("depth") % 2 == 1
    swapped = depth_swap(grid, "depth")
    shares = (ray_offset.astype(jnp.float32) * 0.5)[None, :, None, :]
    occ = expand_blocks(occupancy.astype(jnp.float32))
    first_moment, second_moment, occ = lax.optimization_barrier((first_moment, second_moment, occ))
    plane_out = jnp.where(odd, grid[:, :, 0], grid[:, :, -1])
    feature_grad, plane_in = render(grid, padded[:, 2:], shares, occ, target, total_depth, plane_out)
    plane_before = jnp.where(odd, plane_in, swapped)[:, :, None]
    plane_after = jnp.where(odd, swapped, plane_in)[:, :, None]
    carried = shares * feature_grad
    incoming = passed_along(carried[:, -1:], "tile", 1)
    carried_in = jnp.concatenate([incoming, carried[:, :-1]], axis=1)
    data_grad = (1.0 - shares) * feature_grad + carried_in
    across_rows = padded[:, 2:] + padded[:, :-2]
    across_planes = jnp.concatenate([grid[:, :, 1:], plane_after], axis=2) + jnp.concatenate(
        [plane_before, grid[:, :, :-1]], axis=2
    )
    side_pad = jnp.pad(grid, ((0, 0), (0, 0), (0, 0), (1, 1)))
    across_cols = side_pad[:, :, :, 2:] + side_pad[:, :, :, :-2]
    smooth_grad = 2.0 * tv_weight * (6.0 * grid - across_rows - across_planes - across_cols)
    grad = data_grad + smooth_grad
    new_first = beta_one * first_moment + (1.0 - beta_one) * grad
    new_second = beta_two * second_moment + (1.0 - beta_two) * grad * grad
    corr_one = 1.0 - beta_one**adam_step
    corr_two = 1.0 - beta_two**adam_step
    new_grid = grid - learn_rate * (new_first / corr_one) / (
        jnp.sqrt(new_second / corr_two) + epsilon
    )
    return (new_grid, new_first, new_second)


def solution(mesh):
    in_specs = (
        P(None, "tile", "depth", None),
        P(None, "tile", "depth", None),
        P(None, "tile", "depth", None),
        P("tile", None),
        P("tile", "depth", None),
        P(None, "tile", None),
    )
    out_specs = (
        P(None, "tile", "depth", None),
        P(None, "tile", "depth", None),
        P(None, "tile", "depth", None),
    )
    return jax.shard_map(body, mesh=mesh, in_specs=in_specs, out_specs=out_specs, check_vma=False)
```
